128 devices in a mesh: layer: 2 (over z_hi), row: 8 (over y, core), col: 8 (over z_lo, x).
Axes of the slice: x: 4, y: 4, z: 4 (z_hi: 2, z_lo: 2; z = z_hi * 2 + z_lo), core: 2. Of those that a mesh axis runs over, the one named last changes fastest.
Arguments:
- density: bfloat16 [6400, 6400], P('row', 'col'), may hold values from -2 to 2
- density_mask: int32 [64, 64], P('row', 'col'), may hold values 0 or 1
- square_mask: int32 [64, 64], P('row', 'col'), may hold values 0 or 1
- result_mask: int32 [64, 64], P('row', 'col'), may hold values 0 or 1
- block_perm: int32 [64], replicated, may hold values from 0 to 63, as said below
Outputs:
- purified: bfloat16 [6400, 6400], P('row', 'col')
The draws below stay inside these ranges and needn't reach their ends.
Inputs may be any that keep to these rules, and one draw needn't show every extreme that they name: `block_perm`: A permutation of the 64 block indices. For any two aligned groups of 8 indices, exactly 1 indices of the first group are mapped into the second group.
All inputs are finite; a program needn't handle non-finite values. No bound on the sum of `density_mask` or of `square_mask` or of `result_mask` on one device may be relied on, other than what follows from the above.
Results may differ from the reference program's by a relative error of at most 0.0049.
Values may be sent and summed in bfloat16 or wider, within the bound.
No kernel may reach another device: no remote copies, remote signals or barrier semaphores. Data moves between devices by JAX's collectives and lax.ppermute only.
A program may use at most 64 MiB of HBM per device.

```python
import jax
import jax.numpy as jnp

TILE = 8
BLOCKS = 64
ORDER = 6400
SHARE = 1


def draw_density(key, part):
    scale = (ORDER * 0.5) ** (-1.0 / 3.0)
    first = jax.random.fold_in(key, 11)
    values = jax.random.truncated_normal(first, -4.0, 4.0, (ORDER, ORDER), jnp.float32)
    return (values * scale).astype(jnp.bfloat16)


def draw_block_perm(key, part):
    groups = BLOCKS // TILE
    local_keys = jax.random.split(jax.random.fold_in(key, 21), groups)
    place_keys = jax.random.split(jax.random.fold_in(key, 22), groups)
    local_perm = jax.vmap(lambda single: jax.random.permutation(single, TILE))(local_keys).astype(jnp.int32)
    place_perm = jax.vmap(lambda single: jax.random.permutation(single, TILE))(place_keys).astype(jnp.int32)
    source = jnp.arange(groups, dtype=jnp.int32)[:, None]
    target = local_perm // SHARE
    slot_index = source * SHARE + local_perm % SHARE
    position = target * TILE + place_perm[target, slot_index]
    return position.reshape(BLOCKS).astype(jnp.int32)


def touch_ends(values, rng, low, top_value):
    index_at = [jax.random.randint(jax.random.fold_in(rng, axis), (), 0, length) for axis, length in enumerate(values.shape)]
    widest = values.shape.index(max(values.shape))
    next_to = index_at[:widest] + [(index_at[widest] + 1) % values.shape[widest]] + index_at[widest + 1:]
    return values.at[tuple(index_at)].set(low).at[tuple(next_to)].set(top_value)


def setup_inputs(seed: int = 0) -> dict:
    streams_of = jax.random.split(jax.random.key(seed), 6)
    density = draw_density(jax.random.fold_in(streams_of[5], 71), 0)
    density_mask = touch_ends((jax.random.randint(streams_of[1], (BLOCKS, BLOCKS), 0, 2) < 1).astype(jnp.int32), jax.random.fold_in(streams_of[1], 1), 0, 1)
    square_mask = touch_ends((jax.random.randint(streams_of[2], (BLOCKS, BLOCKS), 0, 4) < 3).astype(jnp.int32), jax.random.fold_in(streams_of[2], 1), 0, 1)
    result_mask = touch_ends((jax.random.randint(streams_of[3], (BLOCKS, BLOCKS), 0, 4) < 3).astype(jnp.int32), jax.random.fold_in(streams_of[3], 1), 0, 1)
    block_perm = draw_block_perm(jax.random.fold_in(streams_of[5], 71), 0)
    return {"density": density, "density_mask": density_mask, "square_mask": square_mask, "result_mask": result_mask, "block_perm": block_perm}


def expand_mask(values, pattern):
    count = pattern.shape[0]
    width = values.shape[0] // count
    shaped = values.reshape(count, width, count, width)
    shaped = shaped * pattern[:, None, :, None].astype(values.dtype)
    return shaped.reshape(count * width, count * width)


def reorder_blocks(values, order):
    count = order.shape[0]
    width = values.shape[0] // count
    shaped = values.reshape(count, width, count, width)
    shaped = jnp.take(shaped, order, axis=0)
    shaped = jnp.take(shaped, order, axis=2)
    return shaped.reshape(count * width, count * width)


def reference(density, density_mask, square_mask, result_mask, block_perm):
    masked = expand_mask(density, density_mask)
    inverse = jnp.argsort(block_perm).astype(jnp.int32)
    grid = reorder_blocks(masked, inverse)
    square = expand_mask(jnp.dot(grid, grid, preferred_element_type=jnp.float32), square_mask).astype(jnp.bfloat16)
    cube = jnp.dot(square, grid, preferred_element_type=jnp.float32)
    result = expand_mask(3.0 * square.astype(jnp.float32) - 2.0 * cube, result_mask).astype(jnp.bfloat16)
    return reorder_blocks(result, block_perm.astype(jnp.int32))
```

```python
import jax
import jax.numpy as jnp
from jax import lax
from jax.sharding import PartitionSpec as P


def apply_pattern(values, pattern):
    count = pattern.shape[0]
    rows = values.shape[0] // count
    cols = values.shape[1] // count
    shaped = values.reshape(count, rows, count, cols)
    shaped = shaped * pattern[:, None, :, None].astype(values.dtype)
    return shaped.reshape(count * rows, count * cols)


def group_order(mapping, group, tile_blocks):
    return jnp.argsort(lax.dynamic_slice_in_dim(mapping, group * tile_blocks, tile_blocks))


def source_groups(mapping, group, tile_blocks):
    return lax.dynamic_slice_in_dim(mapping, group * tile_blocks, tile_blocks) // tile_blocks


def per_device(density, density_mask, square_mask, result_mask, block_perm):
    groups = lax.axis_size("row")
    tile_blocks = density_mask.shape[0]
    width = density.shape[0] // tile_blocks
    half = width // lax.axis_size("layer")
    row_id = lax.axis_index("row")
    col_id = lax.axis_index("col")
    layer_id = lax.axis_index("layer")
    inverse = jnp.argsort(block_perm).astype(jnp.int32)

    masked = apply_pattern(density, density_mask)
    shaped = masked.reshape(tile_blocks, width, tile_blocks, width)
    shaped = jnp.take(shaped, group_order(block_perm, row_id, tile_blocks), axis=0)
    shaped = jnp.take(shaped, group_order(block_perm, col_id, tile_blocks), axis=2)
    pieces = shaped.transpose(0, 2, 1, 3).reshape(groups * groups, width, width)
    received = lax.all_to_all(pieces, ("row", "col"), split_axis=0, concat_axis=0, tiled=True)
    shaped = received.reshape(groups, groups, width, width).transpose(0, 2, 1, 3)
    shaped = jnp.take(shaped, source_groups(inverse, row_id, tile_blocks), axis=0)
    shaped = jnp.take(shaped, source_groups(inverse, col_id, tile_blocks), axis=2)
    grid_tile = shaped.reshape(tile_blocks * width, tile_blocks * width)

    grid_half = lax.dynamic_index_in_dim(
        grid_tile.reshape(tile_blocks, 2, half, tile_blocks * width), layer_id, axis=1, keepdims=False
    ).reshape(tile_blocks * half, tile_blocks * width)
    left = lax.all_gather(grid_half, "col", axis=1, tiled=True)
    right = lax.all_gather(grid_tile, "row", axis=0, tiled=True)

    square_acc = jnp.dot(left, right, preferred_element_type=jnp.float32)
    square = apply_pattern(square_acc, square_mask).astype(jnp.bfloat16)

    square_left = lax.all_gather(square, "col", axis=1, tiled=True)
    cube = jnp.dot(square_left, right, preferred_element_type=jnp.float32)
    result = apply_pattern(3.0 * square.astype(jnp.float32) - 2.0 * cube, result_mask).astype(jnp.bfloat16)

    shaped = result.reshape(tile_blocks, half, tile_blocks, width)
    shaped = jnp.take(shaped, group_order(inverse, row_id, tile_blocks), axis=0)
    shaped = jnp.take(shaped, group_order(inverse, col_id, tile_blocks), axis=2)
    pieces = shaped.transpose(0, 2, 1, 3).reshape(groups * groups, half, width)
    pieces = jnp.concatenate([pieces, pieces], axis=0)
    returned = lax.all_to_all(pieces, ("layer", "row", "col"), split_axis=0, concat_axis=0, tiled=True)
    shaped = returned.reshape(2, groups, groups, half, width).transpose(1, 0, 3, 2, 4)
    shaped = shaped.reshape(groups, width, groups, width)
    shaped = jnp.take(shaped, source_groups(block_perm, row_id, tile_blocks), axis=0)
    shaped = jnp.take(shaped, source_groups(block_perm, col_id, tile_blocks), axis=2)
    return shaped.reshape(tile_blocks * width, tile_blocks * width)


def solution(mesh):
    in_specs = (P("row", "col"), P("row", "col"), P("row", "col"), P("row", "col"), P())
    out_specs = P("row", "col")
    return jax.shard_map(
        per_device, mesh=mesh, in_specs=in_specs, out_specs=out_specs, check_vma=False
    )
```

```python
import jax
import jax.numpy as jnp
from jax import lax
from jax.sharding import PartitionSpec as P


def apply_pattern(values, pattern):
    count = pattern.shape[0]
    rows = values.shape[0] // count
    cols = values.shape[1] // count
    shaped = values.reshape(count, rows, count, cols)
    shaped = shaped * pattern[:, None, :, None].astype(values.dtype)
    return shaped.reshape(count * rows, count * cols)


def group_order(mapping, group, tile_blocks):
    return jnp.argsort(lax.dynamic_slice_in_dim(mapping, group * tile_blocks, tile_blocks))


def source_groups(mapping, group, tile_blocks):
    return lax.dynamic_slice_in_dim(mapping, group * tile_blocks, tile_blocks) // tile_blocks


def per_device(density, density_mask, square_mask, result_mask, block_perm):
    groups = lax.axis_size("row")
    tile_blocks = density_mask.shape[0]
    width = density.shape[0] // tile_blocks
    half = width // lax.axis_size("layer")
    row_id = lax.axis_index("row")
    col_id = lax.axis_index("col")
    layer_id = lax.axis_index("layer")
    inverse = jnp.argsort(block_perm).astype(jnp.int32)

    masked = apply_pattern(density, density_mask)
    shaped = masked.reshape(tile_blocks, width, tile_blocks, width)
    shaped = jnp.take(shaped, group_order(block_perm, row_id, tile_blocks), axis=0)
    shaped = jnp.take(shaped, group_order(block_perm, col_id, tile_blocks), axis=2)
    pieces = shaped.transpose(0, 2, 1, 3).reshape(groups * groups, width, width)
    received = lax.all_to_all(pieces, ("row", "col"), split_axis=0, concat_axis=0, tiled=True)
    shaped = received.reshape(groups, groups, width, width).transpose(0, 2, 1, 3)
    shaped = jnp.take(shaped, source_groups(inverse, row_id, tile_blocks), axis=0)
    shaped = jnp.take(shaped, source_groups(inverse, col_id, tile_blocks), axis=2)
    grid_tile = shaped.reshape(tile_blocks * width, tile_blocks * width)

    grid_half = lax.dynamic_index_in_dim(
        grid_tile.reshape(tile_blocks, 2, half, tile_blocks * width), layer_id, axis=1, keepdims=False
    ).reshape(tile_blocks * half, tile_blocks * width)
    left = lax.all_gather(grid_half, "col", axis=0, tiled=False)
    right = lax.all_gather(grid_tile, "row", axis=0, tiled=False)

    square_acc = jnp.einsum("gik,gkj->ij", left, right, preferred_element_type=jnp.float32)
    square = apply_pattern(square_acc, square_mask).astype(jnp.bfloat16)

    square_left = lax.all_gather(square, "col", axis=0, tiled=False)
    cube = jnp.einsum("gik,gkj->ij", square_left, right, preferred_element_type=jnp.float32)
    result = apply_pattern(3.0 * square.astype(jnp.float32) - 2.0 * cube, result_mask).astype(jnp.bfloat16)

    shaped = result.reshape(tile_blocks, half, tile_blocks, width)
    shaped = jnp.take(shaped, group_order(inverse, row_id, tile_blocks), axis=0)
    shaped = jnp.take(shaped, group_order(inverse, col_id, tile_blocks), axis=2)
    pieces = shaped.transpose(0, 2, 1, 3).reshape(groups * groups, half, width)
    pieces = jnp.concatenate([pieces, pieces], axis=0)
    returned = lax.all_to_all(pieces, ("layer", "row", "col"), split_axis=0, concat_axis=0, tiled=True)
    shaped = returned.reshape(2, groups, groups, half, width).transpose(1, 0, 3, 2, 4)
    shaped = shaped.reshape(groups, width, groups, width)
    shaped = jnp.take(shaped, source_groups(block_perm, row_id, tile_blocks), axis=0)
    shaped = jnp.take(shaped, source_groups(block_perm, col_id, tile_blocks), axis=2)
    return shaped.reshape(tile_blocks * width, tile_blocks * width)


def solution(mesh):
    in_specs = (P("row", "col"), P("row", "col"), P("row", "col"), P("row", "col"), P())
    out_specs = P("row", "col")
    return jax.shard_map(
        per_device, mesh=mesh, in_specs=in_specs, out_specs=out_specs, check_vma=False
    )
```

```python
import jax
import jax.numpy as jnp
from jax import lax
from jax.sharding import PartitionSpec as P


def apply_pattern(values, pattern):
    count = pattern.shape[0]
    rows = values.shape[0] // count
    cols = values.shape[1] // count
    shaped = values.reshape(count, rows, count, cols)
    shaped = shaped * pattern[:, None, :, None].astype(values.dtype)
    return shaped.reshape(count * rows, count * cols)


def group_order(mapping, group, tile_blocks):
    return jnp.argsort(lax.dynamic_slice_in_dim(mapping, group * tile_blocks, tile_blocks))


def source_groups(mapping, group, tile_blocks):
    return lax.dynamic_slice_in_dim(mapping, group * tile_blocks, tile_blocks) // tile_blocks


def passed_along(array, axis, by):
    count = lax.axis_size(axis)
    return lax.ppermute(array, axis, [(i, (i + by) % count) for i in range(count)])


def partner_of(array, axis):
    count = lax.axis_size(axis)
    return lax.ppermute(array, axis, [(i, i ^ 1) for i in range(count)])


def gather_rows(tile, row_id):
    groups = lax.axis_size("row")
    chips = groups // 2
    fetched = [tile] + [passed_along(tile, "row", 2 * step) for step in range(1, chips)]
    shared = [partner_of(piece, "row") for piece in fetched]
    partner = row_id ^ 1
    sources = [(row_id - 2 * step) % groups for step in range(chips)]
    sources += [(partner - 2 * step) % groups for step in range(chips)]
    return jnp.stack(fetched + shared), jnp.stack(sources)


def per_device(density, density_mask, square_mask, result_mask, block_perm):
    groups = lax.axis_size("row")
    tile_blocks = density_mask.shape[0]
    width = density.shape[0] // tile_blocks
    half = width // lax.axis_size("layer")
    row_id = lax.axis_index("row")
    col_id = lax.axis_index("col")
    layer_id = lax.axis_index("layer")
    inverse = jnp.argsort(block_perm).astype(jnp.int32)

    masked = apply_pattern(density, density_mask)
    shaped = masked.reshape(tile_blocks, width, tile_blocks, width)
    shaped = jnp.take(shaped, group_order(block_perm, row_id, tile_blocks), axis=0)
    shaped = jnp.take(shaped, group_order(block_perm, col_id, tile_blocks), axis=2)
    pieces = shaped.transpose(0, 2, 1, 3).reshape(groups * groups, width, width)
    received = lax.all_to_all(pieces, ("row", "col"), split_axis=0, concat_axis=0, tiled=True)
    shaped = received.reshape(groups, groups, width, width).transpose(0, 2, 1, 3)
    shaped = jnp.take(shaped, source_groups(inverse, row_id, tile_blocks), axis=0)
    shaped = jnp.take(shaped, source_groups(inverse, col_id, tile_blocks), axis=2)
    grid_tile = shaped.reshape(tile_blocks * width, tile_blocks * width)

    grid_half = lax.dynamic_index_in_dim(
        grid_tile.reshape(tile_blocks, 2, half, tile_blocks * width), layer_id, axis=1, keepdims=False
    ).reshape(tile_blocks * half, tile_blocks * width)
    left = lax.all_gather(grid_half, "col", axis=0, tiled=False)
    right, sources = gather_rows(grid_tile, row_id)
    left = jnp.take(left, sources, axis=0)

    square_acc = jnp.einsum("gik,gkj->ij", left, right, preferred_element_type=jnp.float32)
    square = apply_pattern(square_acc, square_mask).astype(jnp.bfloat16)

    square_left = jnp.take(lax.all_gather(square, "col", axis=0, tiled=False), sources, axis=0)
    cube = jnp.einsum("gik,gkj->ij", square_left, right, preferred_element_type=jnp.float32)
    result = apply_pattern(3.0 * square.astype(jnp.float32) - 2.0 * cube, result_mask).astype(jnp.bfloat16)

    shaped = result.reshape(tile_blocks, half, tile_blocks, width)
    shaped = jnp.take(shaped, group_order(inverse, row_id, tile_blocks), axis=0)
    shaped = jnp.take(shaped, group_order(inverse, col_id, tile_blocks), axis=2)
    pieces = shaped.transpose(0, 2, 1, 3).reshape(groups * groups, half, width)
    pieces = jnp.concatenate([pieces, pieces], axis=0)
    returned = lax.all_to_all(pieces, ("layer", "row", "col"), split_axis=0, concat_axis=0, tiled=True)
    shaped = returned.reshape(2, groups, groups, half, width).transpose(1, 0, 3, 2, 4)
    shaped = shaped.reshape(groups, width, groups, width)
    shaped = jnp.take(shaped, source_groups(block_perm, row_id, tile_blocks), axis=0)
    shaped = jnp.take(shaped, source_groups(block_perm, col_id, tile_blocks), axis=2)
    return shaped.reshape(tile_blocks * width, tile_blocks * width)


def solution(mesh):
    in_specs = (P("row", "col"), P("row", "col"), P("row", "col"), P("row", "col"), P())
    out_specs = P("row", "col")
    return jax.shard_map(
        per_device, mesh=mesh, in_specs=in_specs, out_specs=out_specs, check_vma=False
    )
```

```python
import jax
import jax.numpy as jnp
from jax import lax
from jax.sharding import PartitionSpec as P


def apply_pattern(values, pattern):
    count = pattern.shape[0]
    rows = values.shape[0] // count
    cols = values.shape[1] // count
    shaped = values.reshape(count, rows, count, cols)
    shaped = shaped * pattern[:, None, :, None].astype(values.dtype)
    return shaped.reshape(count * rows, count * cols)


def group_order(mapping, group, tile_blocks):
    return jnp.argsort(lax.dynamic_slice_in_dim(mapping, group * tile_blocks, tile_blocks))


def source_groups(mapping, group, tile_blocks):
    return lax.dynamic_slice_in_dim(mapping, group * tile_blocks, tile_blocks) // tile_blocks


def passed_along(array, axis, by):
    count = lax.axis_size(axis)
    return lax.ppermute(array, axis, [(i, (i + by) % count) for i in range(count)])


def partner_of(array, axis):
    count = lax.axis_size(axis)
    return lax.ppermute(array, axis, [(i, i ^ 1) for i in range(count)])


def gather_rows(tile, row_id):
    groups = lax.axis_size("row")
    size = tile.shape[0]
    below = passed_along(tile, "row", 2)
    above = passed_along(tile, "row", -2)
    far_top = passed_along(below[: size // 2], "row", 2)
    far_bottom = passed_along(above[size // 2 :], "row", -2)
    own = [(row_id, tile, 0), ((row_id - 2) % groups, below, 0), ((row_id + 2) % groups, above, 0),
           ((row_id + 4) % groups, far_top, 0), ((row_id + 4) % groups, far_bottom, size // 2)]
    shared = [((src ^ 1), partner_of(piece, "row"), first) for src, piece, first in own]
    return own + shared


def contract(stack, pieces):
    total = None
    for src, piece, first in pieces:
        factor = lax.dynamic_index_in_dim(stack, src, axis=0, keepdims=False)
        factor = factor[:, first : first + piece.shape[0]]
        part = jnp.dot(factor, piece, preferred_element_type=jnp.float32)
        total = part if total is None else total + part
    return total


def per_device(density, density_mask, square_mask, result_mask, block_perm):
    groups = lax.axis_size("row")
    tile_blocks = density_mask.shape[0]
    width = density.shape[0] // tile_blocks
    half = width // lax.axis_size("layer")
    row_id = lax.axis_index("row")
    col_id = lax.axis_index("col")
    layer_id = lax.axis_index("layer")
    inverse = jnp.argsort(block_perm).astype(jnp.int32)

    masked = apply_pattern(density, density_mask)
    shaped = masked.reshape(tile_blocks, width, tile_blocks, width)
    shaped = jnp.take(shaped, group_order(block_perm, row_id, tile_blocks), axis=0)
    shaped = jnp.take(shaped, group_order(block_perm, col_id, tile_blocks), axis=2)
    pieces = shaped.transpose(0, 2, 1, 3).reshape(groups * groups, width, width)
    received = lax.all_to_all(pieces, ("row", "col"), split_axis=0, concat_axis=0, tiled=True)
    shaped = received.reshape(groups, groups, width, width).transpose(0, 2, 1, 3)
    shaped = jnp.take(shaped, source_groups(inverse, row_id, tile_blocks), axis=0)
    shaped = jnp.take(shaped, source_groups(inverse, col_id, tile_blocks), axis=2)
    grid_tile = shaped.reshape(tile_blocks * width, tile_blocks * width)

    grid_half = lax.dynamic_index_in_dim(
        grid_tile.reshape(tile_blocks, 2, half, tile_blocks * width), layer_id, axis=1, keepdims=False
    ).reshape(tile_blocks * half, tile_blocks * width)
    left = lax.all_gather(grid_half, "col", axis=0, tiled=False)
    right = gather_rows(grid_tile, row_id)

    square_acc = contract(left, right)
    square = apply_pattern(square_acc, square_mask).astype(jnp.bfloat16)

    square_left = lax.all_gather(square, "col", axis=0, tiled=False)
    cube = contract(square_left, right)
    result = apply_pattern(3.0 * square.astype(jnp.float32) - 2.0 * cube, result_mask).astype(jnp.bfloat16)

    shaped = result.reshape(tile_blocks, half, tile_blocks, width)
    shaped = jnp.take(shaped, group_order(inverse, row_id, tile_blocks), axis=0)
    shaped = jnp.take(shaped, group_order(inverse, col_id, tile_blocks), axis=2)
    pieces = shaped.transpose(0, 2, 1, 3).reshape(groups * groups, half, width)
    pieces = jnp.concatenate([pieces, pieces], axis=0)
    returned = lax.all_to_all(pieces, ("layer", "row", "col"), split_axis=0, concat_axis=0, tiled=True)
    shaped = returned.reshape(2, groups, groups, half, width).transpose(1, 0, 3, 2, 4)
    shaped = shaped.reshape(groups, width, groups, width)
    shaped = jnp.take(shaped, source_groups(block_perm, row_id, tile_blocks), axis=0)
    shaped = jnp.take(shaped, source_groups(block_perm, col_id, tile_blocks), axis=2)
    return shaped.reshape(tile_blocks * width, tile_blocks * width)


def solution(mesh):
    in_specs = (P("row", "col"), P("row", "col"), P("row", "col"), P("row", "col"), P())
    out_specs = P("row", "col")
    return jax.shard_map(
        per_device, mesh=mesh, in_specs=in_specs, out_specs=out_specs, check_vma=False
    )
```

```python
import jax
import jax.numpy as jnp
from jax import lax
from jax.sharding import PartitionSpec as P


def apply_pattern(values, pattern):
    count = pattern.shape[0]
    rows = values.shape[0] // count
    cols = values.shape[1] // count
    shaped = values.reshape(count, rows, count, cols)
    shaped = shaped * pattern[:, None, :, None].astype(values.dtype)
    return shaped.reshape(count * rows, count * cols)


def group_order(mapping, group, tile_blocks):
    return jnp.argsort(lax.dynamic_slice_in_dim(mapping, group * tile_blocks, tile_blocks))


def source_groups(mapping, group, tile_blocks):
    return lax.dynamic_slice_in_dim(mapping, group * tile_blocks, tile_blocks) // tile_blocks


def passed_along(array, axis, by):
    count = lax.axis_size(axis)
    return lax.ppermute(array, axis, [(i, (i + by) % count) for i in range(count)])


def partner_of(array, axis):
    count = lax.axis_size(axis)
    return lax.ppermute(array, axis, [(i, i ^ 1) for i in range(count)])


def gather_rows(tile, row_id):
    groups = lax.axis_size("row")
    size = tile.shape[0]
    below = passed_along(tile, "row", 2)
    above = passed_along(tile, "row", -2)
    far_top = passed_along(below[: size // 2], "row", 2)
    far_bottom = passed_along(above[size // 2 :], "row", -2)
    own = [(row_id, tile, 0), ((row_id - 2) % groups, below, 0), ((row_id + 2) % groups, above, 0),
           ((row_id + 4) % groups, far_top, 0), ((row_id + 4) % groups, far_bottom, size // 2)]
    shared = [((src ^ 1), partner_of(piece, "row"), first) for src, piece, first in own]
    return own + shared


def plane_move(array, by_x, swap_z):
    count = lax.axis_size("col")
    ring = count // 2
    pairs = []
    for i in range(count):
        z, x = divmod(i, ring)
        pairs.append((i, ((1 - z) if swap_z else z) * ring + (x + by_x) % ring))
    return lax.ppermute(array, "col", pairs)


def gather_cols(piece, col_id):
    count = lax.axis_size("col")
    ring = count // 2
    width = piece.shape[1]
    z, x = col_id // ring, col_id % ring

    def col(dz, dx):
        return ((z + dz) % 2) * ring + (x + dx) % ring

    across = plane_move(piece, 0, True)
    pieces = [(col(0, 0), piece, 0), (col(1, 0), across, 0)]
    for dz, start in ((0, piece), (1, across)):
        after = plane_move(start, 1, False)
        before = plane_move(start, -1, False)
        far_left = plane_move(after[:, : width // 2], 1, False)
        far_right = plane_move(before[:, width // 2 :], -1, False)
        pieces += [(col(dz, -1), after, 0), (col(dz, 1), before, 0),
                   (col(dz, 2), far_left, 0), (col(dz, 2), far_right, width // 2)]
    return pieces


def stack_pieces(pieces, groups):
    size = max(piece.shape[0] for _, piece, _ in pieces)
    stack = jnp.zeros((groups, size, pieces[0][1].shape[1]), pieces[0][1].dtype)
    for src, piece, first in pieces:
        stack = lax.dynamic_update_slice(stack, piece[None], (src, first, 0))
    return stack


def contract_left(pieces, stack):
    total = None
    for src, piece, first in pieces:
        factor = lax.dynamic_index_in_dim(stack, src, axis=0, keepdims=False)
        factor = factor[first : first + piece.shape[1]]
        part = jnp.dot(piece, factor, preferred_element_type=jnp.float32)
        total = part if total is None else total + part
    return total


def contract(stack, pieces):
    total = None
    for src, piece, first in pieces:
        factor = lax.dynamic_index_in_dim(stack, src, axis=0, keepdims=False)
        factor = factor[:, first : first + piece.shape[0]]
        part = jnp.dot(factor, piece, preferred_element_type=jnp.float32)
        total = part if total is None else total + part
    return total


def per_device(density, density_mask, square_mask, result_mask, block_perm):
    groups = lax.axis_size("row")
    tile_blocks = density_mask.shape[0]
    width = density.shape[0] // tile_blocks
    half = width // lax.axis_size("layer")
    row_id = lax.axis_index("row")
    col_id = lax.axis_index("col")
    layer_id = lax.axis_index("layer")
    inverse = jnp.argsort(block_perm).astype(jnp.int32)

    masked = apply_pattern(density, density_mask)
    shaped = masked.reshape(tile_blocks, width, tile_blocks, width)
    shaped = jnp.take(shaped, group_order(block_perm, row_id, tile_blocks), axis=0)
    shaped = jnp.take(shaped, group_order(block_perm, col_id, tile_blocks), axis=2)
    pieces = shaped.transpose(0, 2, 1, 3).reshape(groups * groups, width, width)
    received = lax.all_to_all(pieces, ("row", "col"), split_axis=0, concat_axis=0, tiled=True)
    shaped = received.reshape(groups, groups, width, width).transpose(0, 2, 1, 3)
    shaped = jnp.take(shaped, source_groups(inverse, row_id, tile_blocks), axis=0)
    shaped = jnp.take(shaped, source_groups(inverse, col_id, tile_blocks), axis=2)
    grid_tile = shaped.reshape(tile_blocks * width, tile_blocks * width)

    grid_half = lax.dynamic_index_in_dim(
        grid_tile.reshape(tile_blocks, 2, half, tile_blocks * width), layer_id, axis=1, keepdims=False
    ).reshape(tile_blocks * half, tile_blocks * width)
    left = lax.all_gather(grid_half, "col", axis=0, tiled=False)
    right = gather_rows(grid_tile, row_id)

    square_acc = contract(left, right)
    square = apply_pattern(square_acc, square_mask).astype(jnp.bfloat16)

    right_stack = stack_pieces(right, groups)
    cube = contract_left(gather_cols(square, col_id), right_stack)
    result = apply_pattern(3.0 * square.astype(jnp.float32) - 2.0 * cube, result_mask).astype(jnp.bfloat16)

    shaped = result.reshape(tile_blocks, half, tile_blocks, width)
    shaped = jnp.take(shaped, group_order(inverse, row_id, tile_blocks), axis=0)
    shaped = jnp.take(shaped, group_order(inverse, col_id, tile_blocks), axis=2)
    pieces = shaped.transpose(0, 2, 1, 3).reshape(groups * groups, half, width)
    pieces = jnp.concatenate([pieces, pieces], axis=0)
    returned = lax.all_to_all(pieces, ("layer", "row", "col"), split_axis=0, concat_axis=0, tiled=True)
    shaped = returned.reshape(2, groups, groups, half, width).transpose(1, 0, 3, 2, 4)
    shaped = shaped.reshape(groups, width, groups, width)
    shaped = jnp.take(shaped, source_groups(block_perm, row_id, tile_blocks), axis=0)
    shaped = jnp.take(shaped, source_groups(block_perm, col_id, tile_blocks), axis=2)
    return shaped.reshape(tile_blocks * width, tile_blocks * width)


def solution(mesh):
    in_specs = (P("row", "col"), P("row", "col"), P("row", "col"), P("row", "col"), P())
    out_specs = P("row", "col")
    return jax.shard_map(
        per_device, mesh=mesh, in_specs=in_specs, out_specs=out_specs, check_vma=False
    )
```

```python
import jax
import jax.numpy as jnp
from jax import lax
from jax.sharding import PartitionSpec as P


def apply_pattern(values, pattern):
    count = pattern.shape[0]
    rows = values.shape[0] // count
    cols = values.shape[1] // count
    shaped = values.reshape(count, rows, count, cols)
    shaped = shaped * pattern[:, None, :, None].astype(values.dtype)
    return shaped.reshape(count * rows, count * cols)


def group_order(mapping, group, tile_blocks):
    return jnp.argsort(lax.dynamic_slice_in_dim(mapping, group * tile_blocks, tile_blocks))


def source_groups(mapping, group, tile_blocks):
    return lax.dynamic_slice_in_dim(mapping, group * tile_blocks, tile_blocks) // tile_blocks


def passed_along(array, axis, by):
    count = lax.axis_size(axis)
    return lax.ppermute(array, axis, [(i, (i + by) % count) for i in range(count)])


def partner_of(array, axis):
    count = lax.axis_size(axis)
    return lax.ppermute(array, axis, [(i, i ^ 1) for i in range(count)])


def gather_rows(tile, row_id):
    groups = lax.axis_size("row")
    size = tile.shape[0]
    below = passed_along(tile, "row", 2)
    above = passed_along(tile, "row", -2)
    far_top = passed_along(below[: size // 2], "row", 2)
    far_bottom = passed_along(above[size // 2 :], "row", -2)
    own = [(row_id, tile, 0), ((row_id - 2) % groups, below, 0), ((row_id + 2) % groups, above, 0),
           ((row_id + 4) % groups, far_top, 0), ((row_id + 4) % groups, far_bottom, size // 2)]
    shared = [((src ^ 1), partner_of(piece, "row"), first) for src, piece, first in own]
    return own + shared


def plane_move(array, by_x, swap_z):
    count = lax.axis_size("col")
    ring = count // 2
    pairs = []
    for i in range(count):
        z, x = divmod(i, ring)
        pairs.append((i, ((1 - z) if swap_z else z) * ring + (x + by_x) % ring))
    return lax.ppermute(array, "col", pairs)


def gather_cols(piece, col_id):
    count = lax.axis_size("col")
    ring = count // 2
    width = piece.shape[1]
    z, x = col_id // ring, col_id % ring

    def col(dz, dx):
        return ((z + dz) % 2) * ring + (x + dx) % ring

    across = plane_move(piece, 0, True)
    pieces = [(col(0, 0), piece, 0), (col(1, 0), across, 0)]
    for dz, start in ((0, piece), (1, across)):
        after = plane_move(start, 1, False)
        before = plane_move(start, -1, False)
        far_left = plane_move(after[:, : width // 2], 1, False)
        far_right = plane_move(before[:, width // 2 :], -1, False)
        pieces += [(col(dz, -1), after, 0), (col(dz, 1), before, 0),
                   (col(dz, 2), far_left, 0), (col(dz, 2), far_right, width // 2)]
    return pieces


def stack_pieces(pieces, groups):
    size = max(piece.shape[0] for _, piece, _ in pieces)
    stack = jnp.zeros((groups, size, pieces[0][1].shape[1]), pieces[0][1].dtype)
    for src, piece, first in pieces:
        stack = lax.dynamic_update_slice(stack, piece[None], (src, first, 0))
    return stack


def contract_left(pieces, stack):
    total = None
    for src, piece, first in pieces:
        factor = lax.dynamic_index_in_dim(stack, src, axis=0, keepdims=False)
        factor = factor[first : first + piece.shape[1]]
        part = jnp.dot(piece, factor, preferred_element_type=jnp.float32)
        total = part if total is None else total + part
    return total


def contract(stack, pieces):
    total = None
    for src, piece, first in pieces:
        factor = lax.dynamic_index_in_dim(stack, src, axis=0, keepdims=False)
        factor = factor[:, first : first + piece.shape[0]]
        part = jnp.dot(factor, piece, preferred_element_type=jnp.float32)
        total = part if total is None else total + part
    return total


def per_device(density, density_mask, square_mask, result_mask, block_perm):
    groups = lax.axis_size("row")
    tile_blocks = density_mask.shape[0]
    width = density.shape[0] // tile_blocks
    half = width // lax.axis_size("layer")
    row_id = lax.axis_index("row")
    col_id = lax.axis_index("col")
    layer_id = lax.axis_index("layer")
    inverse = jnp.argsort(block_perm).astype(jnp.int32)

    masked = apply_pattern(density, density_mask)
    shaped = lax.dynamic_index_in_dim(
        masked.reshape(tile_blocks, 2, half, tile_blocks * width), layer_id, axis=1, keepdims=False
    )
    shaped = jnp.take(shaped, group_order(block_perm, row_id, tile_blocks), axis=0)
    shaped = lax.all_to_all(shaped, "row", split_axis=0, concat_axis=0, tiled=True)
    shaped = jnp.take(shaped, source_groups(inverse, row_id, tile_blocks), axis=0)
    grid_half = shaped.reshape(tile_blocks * half, tile_blocks * width)

    shaped = masked.reshape(tile_blocks * width, tile_blocks, width)
    shaped = jnp.take(shaped, group_order(block_perm, col_id, tile_blocks), axis=1).transpose(1, 0, 2)
    shaped = lax.all_to_all(shaped, "col", split_axis=0, concat_axis=0, tiled=True)
    shaped = jnp.take(shaped, source_groups(inverse, col_id, tile_blocks), axis=0).transpose(1, 0, 2)
    column_tile = shaped.reshape(tile_blocks * width, tile_blocks * width)

    left = lax.all_gather(grid_half, "col", axis=0, tiled=False)
    right = gather_rows(column_tile, row_id)

    square_acc = contract(left, right)
    square = apply_pattern(square_acc, square_mask).astype(jnp.bfloat16)

    right_stack = stack_pieces(right, groups).reshape(groups * tile_blocks, width, tile_blocks * width)
    right_stack = jnp.take(right_stack, inverse, axis=0).reshape(groups, tile_blocks * width, tile_blocks * width)
    cube = contract_left(gather_cols(square, col_id), right_stack)
    result = apply_pattern(3.0 * square.astype(jnp.float32) - 2.0 * cube, result_mask).astype(jnp.bfloat16)

    shaped = result.reshape(tile_blocks, half, tile_blocks, width)
    shaped = jnp.take(shaped, group_order(inverse, row_id, tile_blocks), axis=0)
    shaped = jnp.take(shaped, group_order(inverse, col_id, tile_blocks), axis=2)
    pieces = shaped.transpose(0, 2, 1, 3).reshape(groups * groups, half, width)
    pieces = jnp.concatenate([pieces, pieces], axis=0)
    returned = lax.all_to_all(pieces, ("layer", "row", "col"), split_axis=0, concat_axis=0, tiled=True)
    shaped = returned.reshape(2, groups, groups, half, width).transpose(1, 0, 3, 2, 4)
    shaped = shaped.reshape(groups, width, groups, width)
    shaped = jnp.take(shaped, source_groups(block_perm, row_id, tile_blocks), axis=0)
    shaped = jnp.take(shaped, source_groups(block_perm, col_id, tile_blocks), axis=2)
    return shaped.reshape(tile_blocks * width, tile_blocks * width)


def solution(mesh):
    in_specs = (P("row", "col"), P("row", "col"), P("row", "col"), P("row", "col"), P())
    out_specs = P("row", "col")
    return jax.shard_map(
        per_device, mesh=mesh, in_specs=in_specs, out_specs=out_specs, check_vma=False
    )
```

```python
import jax
import jax.numpy as jnp
from jax import lax
from jax.sharding import PartitionSpec as P


def apply_pattern(values, pattern):
    count = pattern.shape[0]
    rows = values.shape[0] // count
    cols = values.shape[1] // count
    shaped = values.reshape(count, rows, count, cols)
    shaped = shaped * pattern[:, None, :, None].astype(values.dtype)
    return shaped.reshape(count * rows, count * cols)


def group_order(mapping, group, tile_blocks):
    return jnp.argsort(lax.dynamic_slice_in_dim(mapping, group * tile_blocks, tile_blocks))


def source_groups(mapping, group, tile_blocks):
    return lax.dynamic_slice_in_dim(mapping, group * tile_blocks, tile_blocks) // tile_blocks


def passed_along(array, axis, by):
    count = lax.axis_size(axis)
    return lax.ppermute(array, axis, [(i, (i + by) % count) for i in range(count)])


def partner_of(array, axis):
    count = lax.axis_size(axis)
    return lax.ppermute(array, axis, [(i, i ^ 1) for i in range(count)])


def gather_rows(tile, row_id):
    groups = lax.axis_size("row")
    size = tile.shape[0]
    below = passed_along(tile, "row", 2)
    above = passed_along(tile, "row", -2)
    far_top = passed_along(below[: size // 2], "row", 2)
    far_bottom = passed_along(above[size // 2 :], "row", -2)
    own = [(row_id, tile, 0), ((row_id - 2) % groups, below, 0), ((row_id + 2) % groups, above, 0),
           ((row_id + 4) % groups, far_top, 0), ((row_id + 4) % groups, far_bottom, size // 2)]
    shared = [((src ^ 1), partner_of(piece, "row"), first) for src, piece, first in own]
    return own + shared


def plane_move(array, by_x, swap_z):
    count = lax.axis_size("col")
    ring = count // 2
    pairs = []
    for i in range(count):
        z, x = divmod(i, ring)
        pairs.append((i, ((1 - z) if swap_z else z) * ring + (x + by_x) % ring))
    return lax.ppermute(array, "col", pairs)


def gather_cols(piece, col_id):
    count = lax.axis_size("col")
    ring = count // 2
    width = piece.shape[1]
    z, x = col_id // ring, col_id % ring

    def col(dz, dx):
        return ((z + dz) % 2) * ring + (x + dx) % ring

    across = plane_move(piece, 0, True)
    pieces = [(col(0, 0), piece, 0), (col(1, 0), across, 0)]
    for dz, start in ((0, piece), (1, across)):
        after = plane_move(start, 1, False)
        before = plane_move(start, -1, False)
        far_left = plane_move(after[:, : width // 2], 1, False)
        far_right = plane_move(before[:, width // 2 :], -1, False)
        pieces += [(col(dz, -1), after, 0), (col(dz, 1), before, 0),
                   (col(dz, 2), far_left, 0), (col(dz, 2), far_right, width // 2)]
    return pieces


def stack_pieces(pieces, groups):
    size = max(piece.shape[0] for _, piece, _ in pieces)
    stack = jnp.zeros((groups, size, pieces[0][1].shape[1]), pieces[0][1].dtype)
    for src, piece, first in pieces:
        stack = lax.dynamic_update_slice(stack, piece[None], (src, first, 0))
    return stack


def contract_left(pieces, stack):
    total = None
    for src, piece, first in pieces:
        factor = lax.dynamic_index_in_dim(stack, src, axis=0, keepdims=False)
        factor = factor[first : first + piece.shape[1]]
        part = jnp.dot(piece, factor, preferred_element_type=jnp.float32)
        total = part if total is None else total + part
    return total


def contract(stack, pieces):
    total = None
    for src, piece, first in pieces:
        factor = lax.dynamic_index_in_dim(stack, src, axis=0, keepdims=False)
        factor = factor[:, first : first + piece.shape[0]]
        part = jnp.dot(factor, piece, preferred_element_type=jnp.float32)
        total = part if total is None else total + part
    return total


def per_device(density, density_mask, square_mask, result_mask, block_perm):
    groups = lax.axis_size("row")
    tile_blocks = density_mask.shape[0]
    width = density.shape[0] // tile_blocks
    half = width // lax.axis_size("layer")
    row_id = lax.axis_index("row")
    col_id = lax.axis_index("col")
    layer_id = lax.axis_index("layer")
    inverse = jnp.argsort(block_perm).astype(jnp.int32)

    masked = apply_pattern(density, density_mask)
    shaped = masked.reshape(tile_blocks, width, tile_blocks, width)
    shaped = jnp.take(shaped, group_order(block_perm, row_id, tile_blocks), axis=0)
    shaped = jnp.take(shaped, group_order(block_perm, col_id, tile_blocks), axis=2)
    pieces = shaped.transpose(0, 2, 1, 3).reshape(groups * groups, width, width)
    received = lax.all_to_all(pieces, ("row", "col"), split_axis=0, concat_axis=0, tiled=True)
    shaped = received.reshape(groups, groups, width, width).transpose(0, 2, 1, 3)
    shaped = jnp.take(shaped, source_groups(inverse, row_id, tile_blocks), axis=0)
    shaped = jnp.take(shaped, source_groups(inverse, col_id, tile_blocks), axis=2)
    grid_tile = shaped.reshape(tile_blocks * width, tile_blocks * width)

    grid_half = lax.dynamic_index_in_dim(
        grid_tile.reshape(tile_blocks, 2, half, tile_blocks * width), layer_id, axis=1, keepdims=False
    ).reshape(tile_blocks * half, tile_blocks * width)
    left = lax.all_gather(grid_half, "col", axis=0, tiled=False)
    right = gather_rows(grid_tile, row_id)

    square_acc = contract(left, right)
    square = apply_pattern(square_acc, square_mask).astype(jnp.bfloat16)

    right_stack = stack_pieces(right, groups)
    cube = contract_left(gather_cols(square, col_id), right_stack)
    result = apply_pattern(3.0 * square.astype(jnp.float32) - 2.0 * cube, result_mask).astype(jnp.bfloat16)

    shaped = result.reshape(tile_blocks, half, tile_blocks, width)
    shaped = jnp.take(shaped, group_order(inverse, row_id, tile_blocks), axis=0)
    shaped = jnp.take(shaped, group_order(inverse, col_id, tile_blocks), axis=2)
    pieces = shaped.transpose(0, 2, 1, 3).reshape(groups * groups, half, width)
    mine = lax.all_to_all(pieces, ("row", "col"), split_axis=0, concat_axis=0, tiled=True)
    other = lax.ppermute(mine, "layer", [(0, 1), (1, 0)])
    on_top = layer_id == 0
    returned = jnp.stack([jnp.where(on_top, mine, other), jnp.where(on_top, other, mine)])
    shaped = returned.reshape(2, groups, groups, half, width).transpose(1, 0, 3, 2, 4)
    shaped = shaped.reshape(groups, width, groups, width)
    shaped = jnp.take(shaped, source_groups(block_perm, row_id, tile_blocks), axis=0)
    shaped = jnp.take(shaped, source_groups(block_perm, col_id, tile_blocks), axis=2)
    return shaped.reshape(tile_blocks * width, tile_blocks * width)


def solution(mesh):
    in_specs = (P("row", "col"), P("row", "col"), P("row", "col"), P("row", "col"), P())
    out_specs = P("row", "col")
    return jax.shard_map(
        per_device, mesh=mesh, in_specs=in_specs, out_specs=out_specs, check_vma=False
    )
```

```python
import jax
import jax.numpy as jnp
from jax import lax
from jax.sharding import PartitionSpec as P


def apply_pattern(values, pattern):
    count = pattern.shape[0]
    rows = values.shape[0] // count
    cols = values.shape[1] // count
    shaped = values.reshape(count, rows, count, cols)
    shaped = shaped * pattern[:, None, :, None].astype(values.dtype)
    return shaped.reshape(count * rows, count * cols)


def group_order(mapping, group, tile_blocks):
    return jnp.argsort(lax.dynamic_slice_in_dim(mapping, group * tile_blocks, tile_blocks))


def source_groups(mapping, group, tile_blocks):
    return lax.dynamic_slice_in_dim(mapping, group * tile_blocks, tile_blocks) // tile_blocks


def passed_along(array, axis, by):
    count = lax.axis_size(axis)
    return lax.ppermute(array, axis, [(i, (i + by) % count) for i in range(count)])


def partner_of(array, axis):
    count = lax.axis_size(axis)
    return lax.ppermute(array, axis, [(i, i ^ 1) for i in range(count)])


def gather_rows(tile, row_id):
    groups = lax.axis_size("row")
    size = tile.shape[0]
    below = passed_along(tile, "row", 2)
    above = passed_along(tile, "row", -2)
    far_top = passed_along(below[: size // 2], "row", 2)
    far_bottom = passed_along(above[size // 2 :], "row", -2)
    own = [(row_id, tile, 0), ((row_id - 2) % groups, below, 0), ((row_id + 2) % groups, above, 0),
           ((row_id + 4) % groups, far_top, 0), ((row_id + 4) % groups, far_bottom, size // 2)]
    shared = [((src ^ 1), partner_of(piece, "row"), first) for src, piece, first in own]
    return own + shared


def plane_move(array, by_x, swap_z):
    count = lax.axis_size("col")
    ring = count // 2
    pairs = []
    for i in range(count):
        z, x = divmod(i, ring)
        pairs.append((i, ((1 - z) if swap_z else z) * ring + (x + by_x) % ring))
    return lax.ppermute(array, "col", pairs)


def gather_cols(piece, col_id):
    count = lax.axis_size("col")
    ring = count // 2
    width = piece.shape[1]
    z, x = col_id // ring, col_id % ring

    def col(dz, dx):
        return ((z + dz) % 2) * ring + (x + dx) % ring

    across = plane_move(piece, 0, True)
    pieces = [(col(0, 0), piece, 0), (col(1, 0), across, 0)]
    for dz, start in ((0, piece), (1, across)):
        after = plane_move(start, 1, False)
        before = plane_move(start, -1, False)
        far_left = plane_move(after[:, : width // 2], 1, False)
        far_right = plane_move(before[:, width // 2 :], -1, False)
        pieces += [(col(dz, -1), after, 0), (col(dz, 1), before, 0),
                   (col(dz, 2), far_left, 0), (col(dz, 2), far_right, width // 2)]
    return pieces


def stack_pieces(pieces, groups):
    size = max(piece.shape[0] for _, piece, _ in pieces)
    stack = jnp.zeros((groups, size, pieces[0][1].shape[1]), pieces[0][1].dtype)
    for src, piece, first in pieces:
        stack = lax.dynamic_update_slice(stack, piece[None], (src, first, 0))
    return stack


def contract_left(pieces, stack):
    total = None
    for src, piece, first in pieces:
        factor = lax.dynamic_index_in_dim(stack, src, axis=0, keepdims=False)
        factor = factor[first : first + piece.shape[1]]
        part = jnp.dot(piece, factor, preferred_element_type=jnp.float32)
        total = part if total is None else total + part
    return total


def contract_split(pieces, stacks):
    total = None
    for src, piece, first in pieces:
        width = piece.shape[1]
        for start, stack in stacks:
            low = max(first, start)
            high = min(first + width, start + stack.shape[1])
            if low >= high:
                continue
            factor = lax.dynamic_index_in_dim(stack, src, axis=0, keepdims=False)[low - start : high - start]
            part = jnp.dot(piece[:, low - first : high - first], factor, preferred_element_type=jnp.float32)
            total = part if total is None else total + part
    return total


def contract(stack, pieces):
    total = None
    for src, piece, first in pieces:
        factor = lax.dynamic_index_in_dim(stack, src, axis=0, keepdims=False)
        factor = factor[:, first : first + piece.shape[0]]
        part = jnp.dot(factor, piece, preferred_element_type=jnp.float32)
        total = part if total is None else total + part
    return total


def per_device(density, density_mask, square_mask, result_mask, block_perm):
    groups = lax.axis_size("row")
    tile_blocks = density_mask.shape[0]
    width = density.shape[0] // tile_blocks
    half = width // lax.axis_size("layer")
    row_id = lax.axis_index("row")
    col_id = lax.axis_index("col")
    layer_id = lax.axis_index("layer")
    inverse = jnp.argsort(block_perm).astype(jnp.int32)

    masked = apply_pattern(density, density_mask)
    shaped = masked.reshape(tile_blocks, width, tile_blocks, width)
    shaped = jnp.take(shaped, group_order(block_perm, row_id, tile_blocks), axis=0)
    shaped = jnp.take(shaped, group_order(block_perm, col_id, tile_blocks), axis=2)
    pieces = shaped.transpose(0, 2, 1, 3).reshape(groups * groups, width, width)
    received = lax.all_to_all(pieces, ("row", "col"), split_axis=0, concat_axis=0, tiled=True)
    shaped = received.reshape(groups, groups, width, width).transpose(0, 2, 1, 3)
    shaped = jnp.take(shaped, source_groups(inverse, row_id, tile_blocks), axis=0)
    shaped = jnp.take(shaped, source_groups(inverse, col_id, tile_blocks), axis=2)
    grid_tile = shaped.reshape(tile_blocks * width, tile_blocks * width)

    grid_half = lax.dynamic_index_in_dim(
        grid_tile.reshape(tile_blocks, 2, half, tile_blocks * width), layer_id, axis=1, keepdims=False
    ).reshape(tile_blocks * half, tile_blocks * width)
    size = grid_tile.shape[0]
    right = [(0, lax.all_gather(grid_tile[: size // 2], "row", axis=0, tiled=False)),
             (size // 2, lax.all_gather(grid_tile[size // 2 :], "row", axis=0, tiled=False))]
    left = gather_cols(grid_half, col_id)

    square_acc = contract_split(left, right)
    square = apply_pattern(square_acc, square_mask).astype(jnp.bfloat16)

    cube = contract_split(gather_cols(square, col_id), right)
    result = apply_pattern(3.0 * square.astype(jnp.float32) - 2.0 * cube, result_mask).astype(jnp.bfloat16)

    shaped = result.reshape(tile_blocks, half, tile_blocks, width)
    shaped = jnp.take(shaped, group_order(inverse, row_id, tile_blocks), axis=0)
    shaped = jnp.take(shaped, group_order(inverse, col_id, tile_blocks), axis=2)
    pieces = shaped.transpose(0, 2, 1, 3).reshape(groups * groups, half, width)
    pieces = jnp.concatenate([pieces, pieces], axis=0)
    returned = lax.all_to_all(pieces, ("layer", "row", "col"), split_axis=0, concat_axis=0, tiled=True)
    shaped = returned.reshape(2, groups, groups, half, width).transpose(1, 0, 3, 2, 4)
    shaped = shaped.reshape(groups, width, groups, width)
    shaped = jnp.take(shaped, source_groups(block_perm, row_id, tile_blocks), axis=0)
    shaped = jnp.take(shaped, source_groups(block_perm, col_id, tile_blocks), axis=2)
    return shaped.reshape(tile_blocks * width, tile_blocks * width)


def solution(mesh):
    in_specs = (P("row", "col"), P("row", "col"), P("row", "col"), P("row", "col"), P())
    out_specs = P("row", "col")
    return jax.shard_map(
        per_device, mesh=mesh, in_specs=in_specs, out_specs=out_specs, check_vma=False
    )
```

```python
import jax
import jax.numpy as jnp
from jax import lax
from jax.sharding import PartitionSpec as P


def apply_pattern(values, pattern):
    count = pattern.shape[0]
    rows = values.shape[0] // count
    cols = values.shape[1] // count
    shaped = values.reshape(count, rows, count, cols)
    shaped = shaped * pattern[:, None, :, None].astype(values.dtype)
    return shaped.reshape(count * rows, count * cols)


def group_order(mapping, group, tile_blocks):
    return jnp.argsort(lax.dynamic_slice_in_dim(mapping, group * tile_blocks, tile_blocks))


def source_groups(mapping, group, tile_blocks):
    return lax.dynamic_slice_in_dim(mapping, group * tile_blocks, tile_blocks) // tile_blocks


def passed_along(array, axis, by):
    count = lax.axis_size(axis)
    return lax.ppermute(array, axis, [(i, (i + by) % count) for i in range(count)])


def partner_of(array, axis):
    count = lax.axis_size(axis)
    return lax.ppermute(array, axis, [(i, i ^ 1) for i in range(count)])


def gather_rows(tile, row_id):
    groups = lax.axis_size("row")
    size = tile.shape[0]
    top, bottom = tile[: size // 2], tile[size // 2 :]
    below_top = passed_along(top, "row", 2)
    below_bottom = passed_along(bottom, "row", 2)
    above_top = passed_along(top, "row", -2)
    above_bottom = passed_along(bottom, "row", -2)
    far_top = passed_along(below_top, "row", 2)
    far_bottom = passed_along(above_bottom, "row", -2)
    own = [(row_id, tile, 0),
           ((row_id - 2) % groups, below_top, 0), ((row_id - 2) % groups, below_bottom, size // 2),
           ((row_id + 2) % groups, above_top, 0), ((row_id + 2) % groups, above_bottom, size // 2),
           ((row_id + 4) % groups, far_top, 0), ((row_id + 4) % groups, far_bottom, size // 2)]
    shared = [((src ^ 1), partner_of(piece, "row"), first) for src, piece, first in own]
    return own + shared


def plane_move(array, by_x, swap_z):
    count = lax.axis_size("col")
    ring = count // 2
    pairs = []
    for i in range(count):
        z, x = divmod(i, ring)
        pairs.append((i, ((1 - z) if swap_z else z) * ring + (x + by_x) % ring))
    return lax.ppermute(array, "col", pairs)


def gather_cols(piece, col_id):
    count = lax.axis_size("col")
    ring = count // 2
    width = piece.shape[1]
    z, x = col_id // ring, col_id % ring

    def col(dz, dx):
        return ((z + dz) % 2) * ring + (x + dx) % ring

    across = plane_move(piece, 0, True)
    pieces = [(col(0, 0), piece, 0), (col(1, 0), across, 0)]
    for dz, start in ((0, piece), (1, across)):
        after = plane_move(start, 1, False)
        before = plane_move(start, -1, False)
        far_left = plane_move(after[:, : width // 2], 1, False)
        far_right = plane_move(before[:, width // 2 :], -1, False)
        pieces += [(col(dz, -1), after, 0), (col(dz, 1), before, 0),
                   (col(dz, 2), far_left, 0), (col(dz, 2), far_right, width // 2)]
    return pieces


def stack_pieces(pieces, groups):
    size = max(piece.shape[0] for _, piece, _ in pieces)
    stack = jnp.zeros((groups, size, pieces[0][1].shape[1]), pieces[0][1].dtype)
    for src, piece, first in pieces:
        stack = lax.dynamic_update_slice(stack, piece[None], (src, first, 0))
    return stack


def contract_left(pieces, stack):
    total = None
    for src, piece, first in pieces:
        factor = lax.dynamic_index_in_dim(stack, src, axis=0, keepdims=False)
        factor = factor[first : first + piece.shape[1]]
        part = jnp.dot(piece, factor, preferred_element_type=jnp.float32)
        total = part if total is None else total + part
    return total


def contract(stack, pieces):
    total = None
    for src, piece, first in pieces:
        factor = lax.dynamic_index_in_dim(stack, src, axis=0, keepdims=False)
        factor = factor[:, first : first + piece.shape[0]]
        part = jnp.dot(factor, piece, preferred_element_type=jnp.float32)
        total = part if total is None else total + part
    return total


def per_device(density, density_mask, square_mask, result_mask, block_perm):
    groups = lax.axis_size("row")
    tile_blocks = density_mask.shape[0]
    width = density.shape[0] // tile_blocks
    half = width // lax.axis_size("layer")
    row_id = lax.axis_index("row")
    col_id = lax.axis_index("col")
    layer_id = lax.axis_index("layer")
    inverse = jnp.argsort(block_perm).astype(jnp.int32)

    masked = apply_pattern(density, density_mask)
    shaped = masked.reshape(tile_blocks, width, tile_blocks, width)
    shaped = jnp.take(shaped, group_order(block_perm, row_id, tile_blocks), axis=0)
    shaped = jnp.take(shaped, group_order(block_perm, col_id, tile_blocks), axis=2)
    pieces = shaped.transpose(0, 2, 1, 3).reshape(groups * groups, width, width)
    received = lax.all_to_all(pieces, ("row", "col"), split_axis=0, concat_axis=0, tiled=True)
    shaped = received.reshape(groups, groups, width, width).transpose(0, 2, 1, 3)
    shaped = jnp.take(shaped, source_groups(inverse, row_id, tile_blocks), axis=0)
    shaped = jnp.take(shaped, source_groups(inverse, col_id, tile_blocks), axis=2)
    grid_tile = shaped.reshape(tile_blocks * width, tile_blocks * width)

    grid_half = lax.dynamic_index_in_dim(
        grid_tile.reshape(tile_blocks, 2, half, tile_blocks * width), layer_id, axis=1, keepdims=False
    ).reshape(tile_blocks * half, tile_blocks * width)
    left = lax.all_gather(grid_half, "col", axis=0, tiled=False)
    right = gather_rows(grid_tile, row_id)

    square_acc = contract(left, right)
    square = apply_pattern(square_acc, square_mask).astype(jnp.bfloat16)

    right_stack = stack_pieces(right, groups)
    cube = contract_left(gather_cols(square, col_id), right_stack)
    result = apply_pattern(3.0 * square.astype(jnp.float32) - 2.0 * cube, result_mask).astype(jnp.bfloat16)

    shaped = result.reshape(tile_blocks, half, tile_blocks, width)
    shaped = jnp.take(shaped, group_order(inverse, row_id, tile_blocks), axis=0)
    shaped = jnp.take(shaped, group_order(inverse, col_id, tile_blocks), axis=2)
    pieces = shaped.transpose(0, 2, 1, 3).reshape(groups * groups, half, width)
    pieces = jnp.concatenate([pieces, pieces], axis=0)
    returned = lax.all_to_all(pieces, ("layer", "row", "col"), split_axis=0, concat_axis=0, tiled=True)
    shaped = returned.reshape(2, groups, groups, half, width).transpose(1, 0, 3, 2, 4)
    shaped = shaped.reshape(groups, width, groups, width)
    shaped = jnp.take(shaped, source_groups(block_perm, row_id, tile_blocks), axis=0)
    shaped = jnp.take(shaped, source_groups(block_perm, col_id, tile_blocks), axis=2)
    return shaped.reshape(tile_blocks * width, tile_blocks * width)


def solution(mesh):
    in_specs = (P("row", "col"), P("row", "col"), P("row", "col"), P("row", "col"), P())
    out_specs = P("row", "col")
    return jax.shard_map(
        per_device, mesh=mesh, in_specs=in_specs, out_specs=out_specs, check_vma=False
    )
```

```python
import jax
import jax.numpy as jnp
from jax import lax
from jax.sharding import PartitionSpec as P


def apply_pattern(values, pattern):
    count = pattern.shape[0]
    rows = values.shape[0] // count
    cols = values.shape[1] // count
    shaped = values.reshape(count, rows, count, cols)
    shaped = shaped * pattern[:, None, :, None].astype(values.dtype)
    return shaped.reshape(count * rows, count * cols)


def inverted(mapping):
    positions = jnp.arange(mapping.shape[0], dtype=mapping.dtype)
    hits = mapping[None, :] == positions[:, None]
    return jnp.sum(jnp.where(hits, positions[None, :], 0), axis=1).astype(mapping.dtype)


def group_order(mapping, group, tile_blocks):
    return inverted(lax.dynamic_slice_in_dim(mapping, group * tile_blocks, tile_blocks) // tile_blocks)


def source_groups(mapping, group, tile_blocks):
    return lax.dynamic_slice_in_dim(mapping, group * tile_blocks, tile_blocks) // tile_blocks


def passed_along(array, axis, by):
    count = lax.axis_size(axis)
    return lax.ppermute(array, axis, [(i, (i + by) % count) for i in range(count)])


def partner_of(array, axis):
    count = lax.axis_size(axis)
    return lax.ppermute(array, axis, [(i, i ^ 1) for i in range(count)])


def gather_rows(tile, row_id):
    groups = lax.axis_size("row")
    size = tile.shape[0]
    below = passed_along(tile, "row", 2)
    above = passed_along(tile, "row", -2)
    far_top = passed_along(below[: size // 2], "row", 2)
    far_bottom = passed_along(above[size // 2 :], "row", -2)
    own = [(row_id, tile, 0), ((row_id - 2) % groups, below, 0), ((row_id + 2) % groups, above, 0),
           ((row_id + 4) % groups, far_top, 0), ((row_id + 4) % groups, far_bottom, size // 2)]
    shared = [((src ^ 1), partner_of(piece, "row"), first) for src, piece, first in own]
    return own + shared


def plane_move(array, by_x, swap_z):
    count = lax.axis_size("col")
    ring = count // 2
    pairs = []
    for i in range(count):
        z, x = divmod(i, ring)
        pairs.append((i, ((1 - z) if swap_z else z) * ring + (x + by_x) % ring))
    return lax.ppermute(array, "col", pairs)


def gather_cols(piece, col_id):
    count = lax.axis_size("col")
    ring = count // 2
    width = piece.shape[1]
    z, x = col_id // ring, col_id % ring

    def col(dz, dx):
        return ((z + dz) % 2) * ring + (x + dx) % ring

    across = plane_move(piece, 0, True)
    pieces = [(col(0, 0), piece, 0), (col(1, 0), across, 0)]
    for dz, start in ((0, piece), (1, across)):
        after = plane_move(start, 1, False)
        before = plane_move(start, -1, False)
        far_left = plane_move(after[:, : width // 2], 1, False)
        far_right = plane_move(before[:, width // 2 :], -1, False)
        pieces += [(col(dz, -1), after, 0), (col(dz, 1), before, 0),
                   (col(dz, 2), far_left, 0), (col(dz, 2), far_right, width // 2)]
    return pieces


def stack_pieces(pieces, groups):
    size = max(piece.shape[0] for _, piece, _ in pieces)
    stack = jnp.zeros((groups, size, pieces[0][1].shape[1]), pieces[0][1].dtype)
    for src, piece, first in pieces:
        stack = lax.dynamic_update_slice(stack, piece[None], (src, first, 0))
    return stack


def contract_left(pieces, stack):
    total = None
    for src, piece, first in pieces:
        factor = lax.dynamic_index_in_dim(stack, src, axis=0, keepdims=False)
        factor = factor[first : first + piece.shape[1]]
        part = jnp.dot(piece, factor, preferred_element_type=jnp.float32)
        total = part if total is None else total + part
    return total


def contract(stack, pieces):
    total = None
    for src, piece, first in pieces:
        factor = lax.dynamic_index_in_dim(stack, src, axis=0, keepdims=False)
        factor = factor[:, first : first + piece.shape[0]]
        part = jnp.dot(factor, piece, preferred_element_type=jnp.float32)
        total = part if total is None else total + part
    return total


def per_device(density, density_mask, square_mask, result_mask, block_perm):
    groups = lax.axis_size("row")
    tile_blocks = density_mask.shape[0]
    width = density.shape[0] // tile_blocks
    half = width // lax.axis_size("layer")
    row_id = lax.axis_index("row")
    col_id = lax.axis_index("col")
    layer_id = lax.axis_index("layer")
    inverse = inverted(block_perm)

    masked = apply_pattern(density, density_mask)
    shaped = masked.reshape(tile_blocks, width, tile_blocks, width)
    shaped = jnp.take(shaped, group_order(block_perm, row_id, tile_blocks), axis=0)
    shaped = jnp.take(shaped, group_order(block_perm, col_id, tile_blocks), axis=2)
    pieces = shaped.transpose(0, 2, 1, 3).reshape(groups * groups, width, width)
    received = lax.all_to_all(pieces, ("row", "col"), split_axis=0, concat_axis=0, tiled=True)
    shaped = received.reshape(groups, groups, width, width).transpose(0, 2, 1, 3)
    shaped = jnp.take(shaped, source_groups(inverse, row_id, tile_blocks), axis=0)
    shaped = jnp.take(shaped, source_groups(inverse, col_id, tile_blocks), axis=2)
    grid_tile = shaped.reshape(tile_blocks * width, tile_blocks * width)

    grid_half = lax.dynamic_index_in_dim(
        grid_tile.reshape(tile_blocks, 2, half, tile_blocks * width), layer_id, axis=1, keepdims=False
    ).reshape(tile_blocks * half, tile_blocks * width)
    left = lax.all_gather(grid_half, "col", axis=0, tiled=False)
    right = gather_rows(grid_tile, row_id)

    square_acc = contract(left, right)
    square = apply_pattern(square_acc, square_mask).astype(jnp.bfloat16)

    right_stack = stack_pieces(right, groups)
    cube = contract_left(gather_cols(square, col_id), right_stack)
    result = apply_pattern(3.0 * square.astype(jnp.float32) - 2.0 * cube, result_mask).astype(jnp.bfloat16)

    shaped = result.reshape(tile_blocks, half, tile_blocks, width)
    shaped = jnp.take(shaped, group_order(inverse, row_id, tile_blocks), axis=0)
    shaped = jnp.take(shaped, group_order(inverse, col_id, tile_blocks), axis=2)
    pieces = shaped.transpose(0, 2, 1, 3).reshape(groups * groups, half, width)
    pieces = jnp.concatenate([pieces, pieces], axis=0)
    returned = lax.all_to_all(pieces, ("layer", "row", "col"), split_axis=0, concat_axis=0, tiled=True)
    shaped = returned.reshape(2, groups, groups, half, width).transpose(1, 0, 3, 2, 4)
    shaped = shaped.reshape(groups, width, groups, width)
    shaped = jnp.take(shaped, source_groups(block_perm, row_id, tile_blocks), axis=0)
    shaped = jnp.take(shaped, source_groups(block_perm, col_id, tile_blocks), axis=2)
    return shaped.reshape(tile_blocks * width, tile_blocks * width)


def solution(mesh):
    in_specs = (P("row", "col"), P("row", "col"), P("row", "col"), P("row", "col"), P())
    out_specs = P("row", "col")
    return jax.shard_map(
        per_device, mesh=mesh, in_specs=in_specs, out_specs=out_specs, check_vma=False
    )
```

```python
import jax
import jax.numpy as jnp
from jax import lax
from jax.sharding import PartitionSpec as P


def apply_pattern(values, pattern):
    count = pattern.shape[0]
    rows = values.shape[0] // count
    cols = values.shape[1] // count
    shaped = values.reshape(count, rows, count, cols)
    shaped = shaped * pattern[:, None, :, None].astype(values.dtype)
    return shaped.reshape(count * rows, count * cols)


def inverted(mapping):
    positions = jnp.arange(mapping.shape[0], dtype=mapping.dtype)
    hits = mapping[None, :] == positions[:, None]
    return jnp.sum(jnp.where(hits, positions[None, :], 0), axis=1).astype(mapping.dtype)


def group_order(mapping, group, tile_blocks):
    return inverted(lax.dynamic_slice_in_dim(mapping, group * tile_blocks, tile_blocks) // tile_blocks)


def source_groups(mapping, group, tile_blocks):
    return lax.dynamic_slice_in_dim(mapping, group * tile_blocks, tile_blocks) // tile_blocks


def passed_along(array, axis, by):
    count = lax.axis_size(axis)
    return lax.ppermute(array, axis, [(i, (i + by) % count) for i in range(count)])


def partner_of(array, axis):
    count = lax.axis_size(axis)
    return lax.ppermute(array, axis, [(i, i ^ 1) for i in range(count)])


def gather_rows(tile, row_id):
    groups = lax.axis_size("row")
    size = tile.shape[0]
    below = passed_along(tile, "row", 2)
    above = passed_along(tile, "row", -2)
    far_top = passed_along(below[: size // 2], "row", 2)
    far_bottom = passed_along(above[size // 2 :], "row", -2)
    own = [(row_id, tile, 0), ((row_id - 2) % groups, below, 0), ((row_id + 2) % groups, above, 0),
           ((row_id + 4) % groups, far_top, 0), ((row_id + 4) % groups, far_bottom, size // 2)]
    shared = [((src ^ 1), partner_of(piece, "row"), first) for src, piece, first in own]
    return own + shared


def plane_move(array, by_x, swap_z):
    count = lax.axis_size("col")
    ring = count // 2
    pairs = []
    for i in range(count):
        z, x = divmod(i, ring)
        pairs.append((i, ((1 - z) if swap_z else z) * ring + (x + by_x) % ring))
    return lax.ppermute(array, "col", pairs)


def gather_cols(piece, col_id):
    count = lax.axis_size("col")
    ring = count // 2
    width = piece.shape[1]
    z, x = col_id // ring, col_id % ring

    def col(dz, dx):
        return ((z + dz) % 2) * ring + (x + dx) % ring

    across = plane_move(piece, 0, True)
    pieces = [(col(0, 0), piece, 0), (col(1, 0), across, 0)]
    for dz, start in ((0, piece), (1, across)):
        after = plane_move(start, 1, False)
        before = plane_move(start, -1, False)
        far_left = plane_move(after[:, : width // 2], 1, False)
        far_right = plane_move(before[:, width // 2 :], -1, False)
        pieces += [(col(dz, -1), after, 0), (col(dz, 1), before, 0),
                   (col(dz, 2), far_left, 0), (col(dz, 2), far_right, width // 2)]
    return pieces


def stack_pieces(pieces, groups):
    size = max(piece.shape[0] for _, piece, _ in pieces)
    stack = jnp.zeros((groups, size, pieces[0][1].shape[1]), pieces[0][1].dtype)
    for src, piece, first in pieces:
        stack = lax.dynamic_update_slice(stack, piece[None], (src, first, 0))
    return stack


def contract_left(pieces, stack):
    total = None
    for src, piece, first in pieces:
        factor = lax.dynamic_index_in_dim(stack, src, axis=0, keepdims=False)
        factor = factor[first : first + piece.shape[1]]
        part = jnp.dot(piece, factor, preferred_element_type=jnp.float32)
        total = part if total is None else total + part
    return total


def contract(stack, pieces):
    total = None
    for src, piece, first in pieces:
        factor = lax.dynamic_index_in_dim(stack, src, axis=0, keepdims=False)
        factor = factor[:, first : first + piece.shape[0]]
        part = jnp.dot(factor, piece, preferred_element_type=jnp.float32)
        total = part if total is None else total + part
    return total


def per_device(density, density_mask, square_mask, result_mask, block_perm):
    groups = lax.axis_size("row")
    tile_blocks = density_mask.shape[0]
    width = density.shape[0] // tile_blocks
    half = width // lax.axis_size("layer")
    row_id = lax.axis_index("row")
    col_id = lax.axis_index("col")
    layer_id = lax.axis_index("layer")
    inverse = inverted(block_perm)

    masked = apply_pattern(density, density_mask)
    shaped = masked.reshape(tile_blocks, width, tile_blocks, width)
    shaped = jnp.take(shaped, group_order(block_perm, row_id, tile_blocks), axis=0)
    shaped = jnp.take(shaped, group_order(block_perm, col_id, tile_blocks), axis=2)
    pieces = shaped.transpose(0, 2, 1, 3).reshape(groups * groups, width, width)
    received = lax.all_to_all(pieces, ("row", "col"), split_axis=0, concat_axis=0, tiled=True)
    shaped = received.reshape(groups, groups, width, width).transpose(0, 2, 1, 3)
    shaped = jnp.take(shaped, source_groups(inverse, row_id, tile_blocks), axis=0)
    shaped = jnp.take(shaped, source_groups(inverse, col_id, tile_blocks), axis=2)
    grid_tile = shaped.reshape(tile_blocks * width, tile_blocks * width)

    grid_half = lax.dynamic_index_in_dim(
        grid_tile.reshape(tile_blocks, 2, half, tile_blocks * width), layer_id, axis=1, keepdims=False
    ).reshape(tile_blocks * half, tile_blocks * width)
    split = grid_half.shape[0] // 2
    left_top = lax.all_gather(grid_half[:split], "col", axis=0, tiled=False)
    left_bottom = lax.all_gather(grid_half[split:], "col", axis=0, tiled=False)
    right = gather_rows(grid_tile, row_id)
    right_stack = stack_pieces(right, groups)

    square_acc = jnp.concatenate(
        [contract(left_top, right),
         jnp.einsum("gik,gkj->ij", left_bottom, right_stack, preferred_element_type=jnp.float32)], axis=0)
    square = apply_pattern(square_acc, square_mask).astype(jnp.bfloat16)

    cube = contract_left(gather_cols(square, col_id), right_stack)
    result = apply_pattern(3.0 * square.astype(jnp.float32) - 2.0 * cube, result_mask).astype(jnp.bfloat16)

    shaped = result.reshape(tile_blocks, half, tile_blocks, width)
    shaped = jnp.take(shaped, group_order(inverse, row_id, tile_blocks), axis=0)
    shaped = jnp.take(shaped, group_order(inverse, col_id, tile_blocks), axis=2)
    pieces = shaped.transpose(0, 2, 1, 3).reshape(groups * groups, half, width)
    pieces = jnp.concatenate([pieces, pieces], axis=0)
    returned = lax.all_to_all(pieces, ("layer", "row", "col"), split_axis=0, concat_axis=0, tiled=True)
    shaped = returned.reshape(2, groups, groups, half, width).transpose(1, 0, 3, 2, 4)
    shaped = shaped.reshape(groups, width, groups, width)
    shaped = jnp.take(shaped, source_groups(block_perm, row_id, tile_blocks), axis=0)
    shaped = jnp.take(shaped, source_groups(block_perm, col_id, tile_blocks), axis=2)
    return shaped.reshape(tile_blocks * width, tile_blocks * width)


def solution(mesh):
    in_specs = (P("row", "col"), P("row", "col"), P("row", "col"), P("row", "col"), P())
    out_specs = P("row", "col")
    return jax.shard_map(
        per_device, mesh=mesh, in_specs=in_specs, out_specs=out_specs, check_vma=False
    )
```

```python
import jax
import jax.numpy as jnp
from jax import lax
from jax.sharding import PartitionSpec as P


def apply_pattern(values, pattern):
    count = pattern.shape[0]
    rows = values.shape[0] // count
    cols = values.shape[1] // count
    shaped = values.reshape(count, rows, count, cols)
    shaped = shaped * pattern[:, None, :, None].astype(values.dtype)
    return shaped.reshape(count * rows, count * cols)


def inverted(mapping):
    positions = jnp.arange(mapping.shape[0], dtype=mapping.dtype)
    hits = mapping[None, :] == positions[:, None]
    return jnp.sum(jnp.where(hits, positions[None, :], 0), axis=1).astype(mapping.dtype)


def group_order(mapping, group, tile_blocks):
    return inverted(lax.dynamic_slice_in_dim(mapping, group * tile_blocks, tile_blocks) // tile_blocks)


def source_groups(mapping, group, tile_blocks):
    return lax.dynamic_slice_in_dim(mapping, group * tile_blocks, tile_blocks) // tile_blocks


def passed_along(array, axis, by):
    count = lax.axis_size(axis)
    return lax.ppermute(array, axis, [(i, (i + by) % count) for i in range(count)])


def partner_of(array, axis):
    count = lax.axis_size(axis)
    return lax.ppermute(array, axis, [(i, i ^ 1) for i in range(count)])


def gather_rows(tile, row_id):
    groups = lax.axis_size("row")
    size = tile.shape[0]
    below = passed_along(tile, "row", 2)
    above = passed_along(tile, "row", -2)
    far_top = passed_along(below[: size // 2], "row", 2)
    far_bottom = passed_along(above[size // 2 :], "row", -2)
    own = [(row_id, tile, 0), ((row_id - 2) % groups, below, 0), ((row_id + 2) % groups, above, 0),
           ((row_id + 4) % groups, far_top, 0), ((row_id + 4) % groups, far_bottom, size // 2)]
    shared = [((src ^ 1), partner_of(piece, "row"), first) for src, piece, first in own]
    return own + shared


def plane_move(array, by_x, swap_z):
    count = lax.axis_size("col")
    ring = count // 2
    pairs = []
    for i in range(count):
        z, x = divmod(i, ring)
        pairs.append((i, ((1 - z) if swap_z else z) * ring + (x + by_x) % ring))
    return lax.ppermute(array, "col", pairs)


def gather_cols(piece, col_id):
    count = lax.axis_size("col")
    ring = count // 2
    width = piece.shape[1]
    z, x = col_id // ring, col_id % ring

    def col(dz, dx):
        return ((z + dz) % 2) * ring + (x + dx) % ring

    across = plane_move(piece, 0, True)
    pieces = [(col(0, 0), piece, 0), (col(1, 0), across, 0)]
    for dz, start in ((0, piece), (1, across)):
        after = plane_move(start, 1, False)
        before = plane_move(start, -1, False)
        far_left = plane_move(after[:, : width // 2], 1, False)
        far_right = plane_move(before[:, width // 2 :], -1, False)
        pieces += [(col(dz, -1), after, 0), (col(dz, 1), before, 0),
                   (col(dz, 2), far_left, 0), (col(dz, 2), far_right, width // 2)]
    return pieces


def stack_pieces(pieces, groups):
    size = max(piece.shape[0] for _, piece, _ in pieces)
    stack = jnp.zeros((groups, size, pieces[0][1].shape[1]), pieces[0][1].dtype)
    for src, piece, first in pieces:
        stack = lax.dynamic_update_slice(stack, piece[None], (src, first, 0))
    return stack


def contract_left(pieces, stack):
    total = None
    for src, piece, first in pieces:
        factor = lax.dynamic_index_in_dim(stack, src, axis=0, keepdims=False)
        factor = factor[first : first + piece.shape[1]]
        part = jnp.dot(piece, factor, preferred_element_type=jnp.float32)
        total = part if total is None else total + part
    return total


def per_device(density, density_mask, square_mask, result_mask, block_perm):
    groups = lax.axis_size("row")
    tile_blocks = density_mask.shape[0]
    width = density.shape[0] // tile_blocks
    half = width // lax.axis_size("layer")
    row_id = lax.axis_index("row")
    col_id = lax.axis_index("col")
    layer_id = lax.axis_index("layer")
    inverse = inverted(block_perm)

    masked = apply_pattern(density, density_mask)
    shaped = masked.reshape(tile_blocks, width, tile_blocks, width)
    shaped = jnp.take(shaped, group_order(block_perm, row_id, tile_blocks), axis=0)
    shaped = jnp.take(shaped, group_order(block_perm, col_id, tile_blocks), axis=2)
    pieces = shaped.transpose(0, 2, 1, 3).reshape(groups * groups, width, width)
    received = lax.all_to_all(pieces, ("row", "col"), split_axis=0, concat_axis=0, tiled=True)
    shaped = received.reshape(groups, groups, width, width).transpose(0, 2, 1, 3)
    shaped = jnp.take(shaped, source_groups(inverse, row_id, tile_blocks), axis=0)
    shaped = jnp.take(shaped, source_groups(inverse, col_id, tile_blocks), axis=2)
    grid_tile = shaped.reshape(tile_blocks * width, tile_blocks * width)

    grid_half = lax.dynamic_index_in_dim(
        grid_tile.reshape(tile_blocks, 2, half, tile_blocks * width), layer_id, axis=1, keepdims=False
    ).reshape(tile_blocks * half, tile_blocks * width)
    left = lax.all_gather(grid_half, "col", axis=0, tiled=False)
    right = gather_rows(grid_tile, row_id)
    right_stack = stack_pieces(right, groups)

    square_acc = jnp.einsum("gik,gkj->ij", left, right_stack, preferred_element_type=jnp.float32)
    square = apply_pattern(square_acc, square_mask).astype(jnp.bfloat16)

    cube = contract_left(gather_cols(square, col_id), right_stack)
    result = apply_pattern(3.0 * square.astype(jnp.float32) - 2.0 * cube, result_mask).astype(jnp.bfloat16)

    shaped = result.reshape(tile_blocks, half, tile_blocks, width)
    shaped = jnp.take(shaped, group_order(inverse, row_id, tile_blocks), axis=0)
    shaped = jnp.take(shaped, group_order(inverse, col_id, tile_blocks), axis=2)
    pieces = shaped.transpose(0, 2, 1, 3).reshape(groups * groups, half, width)
    pieces = jnp.concatenate([pieces, pieces], axis=0)
    returned = lax.all_to_all(pieces, ("layer", "row", "col"), split_axis=0, concat_axis=0, tiled=True)
    shaped = returned.reshape(2, groups, groups, half, width).transpose(1, 0, 3, 2, 4)
    shaped = shaped.reshape(groups, width, groups, width)
    shaped = jnp.take(shaped, source_groups(block_perm, row_id, tile_blocks), axis=0)
    shaped = jnp.take(shaped, source_groups(block_perm, col_id, tile_blocks), axis=2)
    return shaped.reshape(tile_blocks * width, tile_blocks * width)


def solution(mesh):
    in_specs = (P("row", "col"), P("row", "col"), P("row", "col"), P("row", "col"), P())
    out_specs = P("row", "col")
    return jax.shard_map(
        per_device, mesh=mesh, in_specs=in_specs, out_specs=out_specs, check_vma=False
    )
```

```python
import jax
import jax.numpy as jnp
from jax import lax
from jax.sharding import PartitionSpec as P


def apply_pattern(values, pattern):
    count = pattern.shape[0]
    rows = values.shape[0] // count
    cols = values.shape[1] // count
    shaped = values.reshape(count, rows, count, cols)
    shaped = shaped * pattern[:, None, :, None].astype(values.dtype)
    return shaped.reshape(count * rows, count * cols)


def inverted(mapping):
    positions = jnp.arange(mapping.shape[0], dtype=mapping.dtype)
    hits = mapping[None, :] == positions[:, None]
    return jnp.sum(jnp.where(hits, positions[None, :], 0), axis=1).astype(mapping.dtype)


def group_order(mapping, group, tile_blocks):
    return inverted(lax.dynamic_slice_in_dim(mapping, group * tile_blocks, tile_blocks) // tile_blocks)


def source_groups(mapping, group, tile_blocks):
    return lax.dynamic_slice_in_dim(mapping, group * tile_blocks, tile_blocks) // tile_blocks


def passed_along(array, axis, by):
    count = lax.axis_size(axis)
    return lax.ppermute(array, axis, [(i, (i + by) % count) for i in range(count)])


def partner_of(array, axis):
    count = lax.axis_size(axis)
    return lax.ppermute(array, axis, [(i, i ^ 1) for i in range(count)])


def gather_rows(tile, row_id):
    groups = lax.axis_size("row")
    size = tile.shape[0]
    below = passed_along(tile, "row", 2)
    above = passed_along(tile, "row", -2)
    far_top = passed_along(below[: size // 2], "row", 2)
    far_bottom = passed_along(above[size // 2 :], "row", -2)
    own = [(row_id, tile, 0), ((row_id - 2) % groups, below, 0), ((row_id + 2) % groups, above, 0),
           ((row_id + 4) % groups, far_top, 0), ((row_id + 4) % groups, far_bottom, size // 2)]
    shared = [((src ^ 1), partner_of(piece, "row"), first) for src, piece, first in own]
    return own + shared


def plane_move(array, by_x, swap_z):
    count = lax.axis_size("col")
    ring = count // 2
    pairs = []
    for i in range(count):
        z, x = divmod(i, ring)
        pairs.append((i, ((1 - z) if swap_z else z) * ring + (x + by_x) % ring))
    return lax.ppermute(array, "col", pairs)


def gather_cols(piece, col_id):
    count = lax.axis_size("col")
    ring = count // 2
    width = piece.shape[1]
    z, x = col_id // ring, col_id % ring

    def col(dz, dx):
        return ((z + dz) % 2) * ring + (x + dx) % ring

    across = plane_move(piece, 0, True)
    pieces = [(col(0, 0), piece, 0), (col(1, 0), across, 0)]
    for dz, start in ((0, piece), (1, across)):
        after = plane_move(start, 1, False)
        before = plane_move(start, -1, False)
        far_left = plane_move(after[:, : width // 2], 1, False)
        far_right = plane_move(before[:, width // 2 :], -1, False)
        pieces += [(col(dz, -1), after, 0), (col(dz, 1), before, 0),
                   (col(dz, 2), far_left, 0), (col(dz, 2), far_right, width // 2)]
    return pieces


def stack_pieces(pieces, groups):
    size = max(piece.shape[0] for _, piece, _ in pieces)
    stack = jnp.zeros((groups, size, pieces[0][1].shape[1]), pieces[0][1].dtype)
    for src, piece, first in pieces:
        stack = lax.dynamic_update_slice(stack, piece[None], (src, first, 0))
    return stack


def stack_columns(pieces, groups, width):
    stack = jnp.zeros((groups, pieces[0][1].shape[0], width), pieces[0][1].dtype)
    for src, piece, first in pieces:
        stack = lax.dynamic_update_slice(stack, piece[None], (src, 0, first))
    return stack


def contract_left(pieces, stack):
    total = None
    for src, piece, first in pieces:
        factor = lax.dynamic_index_in_dim(stack, src, axis=0, keepdims=False)
        factor = factor[first : first + piece.shape[1]]
        part = jnp.dot(piece, factor, preferred_element_type=jnp.float32)
        total = part if total is None else total + part
    return total


def per_device(density, density_mask, square_mask, result_mask, block_perm):
    groups = lax.axis_size("row")
    tile_blocks = density_mask.shape[0]
    width = density.shape[0] // tile_blocks
    half = width // lax.axis_size("layer")
    row_id = lax.axis_index("row")
    col_id = lax.axis_index("col")
    layer_id = lax.axis_index("layer")
    inverse = inverted(block_perm)

    masked = apply_pattern(density, density_mask)
    shaped = masked.reshape(tile_blocks, width, tile_blocks, width)
    shaped = jnp.take(shaped, group_order(block_perm, row_id, tile_blocks), axis=0)
    shaped = jnp.take(shaped, group_order(block_perm, col_id, tile_blocks), axis=2)
    pieces = shaped.transpose(0, 2, 1, 3).reshape(groups * groups, width, width)
    received = lax.all_to_all(pieces, ("row", "col"), split_axis=0, concat_axis=0, tiled=True)
    shaped = received.reshape(groups, groups, width, width).transpose(0, 2, 1, 3)
    shaped = jnp.take(shaped, source_groups(inverse, row_id, tile_blocks), axis=0)
    shaped = jnp.take(shaped, source_groups(inverse, col_id, tile_blocks), axis=2)
    grid_tile = shaped.reshape(tile_blocks * width, tile_blocks * width)

    grid_half = lax.dynamic_index_in_dim(
        grid_tile.reshape(tile_blocks, 2, half, tile_blocks * width), layer_id, axis=1, keepdims=False
    ).reshape(tile_blocks * half, tile_blocks * width)
    left = stack_columns(gather_cols(grid_half, col_id), groups, grid_half.shape[1])
    right = gather_rows(grid_tile, row_id)
    right_stack = stack_pieces(right, groups)

    square_acc = jnp.einsum("gik,gkj->ij", left, right_stack, preferred_element_type=jnp.float32)
    square = apply_pattern(square_acc, square_mask).astype(jnp.bfloat16)

    cube = contract_left(gather_cols(square, col_id), right_stack)
    result = apply_pattern(3.0 * square.astype(jnp.float32) - 2.0 * cube, result_mask).astype(jnp.bfloat16)

    shaped = result.reshape(tile_blocks, half, tile_blocks, width)
    shaped = jnp.take(shaped, group_order(inverse, row_id, tile_blocks), axis=0)
    shaped = jnp.take(shaped, group_order(inverse, col_id, tile_blocks), axis=2)
    pieces = shaped.transpose(0, 2, 1, 3).reshape(groups * groups, half, width)
    pieces = jnp.concatenate([pieces, pieces], axis=0)
    returned = lax.all_to_all(pieces, ("layer", "row", "col"), split_axis=0, concat_axis=0, tiled=True)
    shaped = returned.reshape(2, groups, groups, half, width).transpose(1, 0, 3, 2, 4)
    shaped = shaped.reshape(groups, width, groups, width)
    shaped = jnp.take(shaped, source_groups(block_perm, row_id, tile_blocks), axis=0)
    shaped = jnp.take(shaped, source_groups(block_perm, col_id, tile_blocks), axis=2)
    return shaped.reshape(tile_blocks * width, tile_blocks * width)


def solution(mesh):
    in_specs = (P("row", "col"), P("row", "col"), P("row", "col"), P("row", "col"), P())
    out_specs = P("row", "col")
    return jax.shard_map(
        per_device, mesh=mesh, in_specs=in_specs, out_specs=out_specs, check_vma=False
    )
```

```python
import jax
import jax.numpy as jnp
from jax import lax
from jax.sharding import PartitionSpec as P


def apply_pattern(values, pattern):
    count = pattern.shape[0]
    rows = values.shape[0] // count
    cols = values.shape[1] // count
    shaped = values.reshape(count, rows, count, cols)
    shaped = shaped * pattern[:, None, :, None].astype(values.dtype)
    return shaped.reshape(count * rows, count * cols)


def inverted(mapping):
    positions = jnp.arange(mapping.shape[0], dtype=mapping.dtype)
    hits = mapping[None, :] == positions[:, None]
    return jnp.sum(jnp.where(hits, positions[None, :], 0), axis=1).astype(mapping.dtype)


def group_order(mapping, group, tile_blocks):
    return inverted(lax.dynamic_slice_in_dim(mapping, group * tile_blocks, tile_blocks) // tile_blocks)


def source_groups(mapping, group, tile_blocks):
    return lax.dynamic_slice_in_dim(mapping, group * tile_blocks, tile_blocks) // tile_blocks


def passed_along(array, axis, by):
    count = lax.axis_size(axis)
    return lax.ppermute(array, axis, [(i, (i + by) % count) for i in range(count)])


def partner_of(array, axis):
    count = lax.axis_size(axis)
    return lax.ppermute(array, axis, [(i, i ^ 1) for i in range(count)])


def gather_rows(tile, row_id):
    groups = lax.axis_size("row")
    size = tile.shape[0]
    below = passed_along(tile, "row", 2)
    above = passed_along(tile, "row", -2)
    far_top = passed_along(below[: size // 2], "row", 2)
    far_bottom = passed_along(above[size // 2 :], "row", -2)
    own = [(row_id, tile, 0), ((row_id - 2) % groups, below, 0), ((row_id + 2) % groups, above, 0),
           ((row_id + 4) % groups, far_top, 0), ((row_id + 4) % groups, far_bottom, size // 2)]
    shared = [((src ^ 1), partner_of(piece, "row"), first) for src, piece, first in own]
    return own + shared


def plane_move(array, by_x, swap_z):
    count = lax.axis_size("col")
    ring = count // 2
    pairs = []
    for i in range(count):
        z, x = divmod(i, ring)
        pairs.append((i, ((1 - z) if swap_z else z) * ring + (x + by_x) % ring))
    return lax.ppermute(array, "col", pairs)


def gather_cols(piece, col_id):
    count = lax.axis_size("col")
    ring = count // 2
    width = piece.shape[1]
    z, x = col_id // ring, col_id % ring

    def col(dz, dx):
        return ((z + dz) % 2) * ring + (x + dx) % ring

    across = plane_move(piece, 0, True)
    pieces = [(col(0, 0), piece, 0), (col(1, 0), across, 0)]
    for dz, start in ((0, piece), (1, across)):
        after = plane_move(start, 1, False)
        before = plane_move(start, -1, False)
        far_left = plane_move(after[:, : width // 2], 1, False)
        far_right = plane_move(before[:, width // 2 :], -1, False)
        pieces += [(col(dz, -1), after, 0), (col(dz, 1), before, 0),
                   (col(dz, 2), far_left, 0), (col(dz, 2), far_right, width // 2)]
    return pieces


def stack_pieces(pieces, groups):
    size = max(piece.shape[0] for _, piece, _ in pieces)
    stack = jnp.zeros((groups, size, pieces[0][1].shape[1]), pieces[0][1].dtype)
    for src, piece, first in pieces:
        stack = lax.dynamic_update_slice(stack, piece[None], (src, first, 0))
    return stack


def contract_left(pieces, stack):
    total = None
    for src, piece, first in pieces:
        factor = lax.dynamic_index_in_dim(stack, src, axis=0, keepdims=False)
        factor = factor[first : first + piece.shape[1]]
        part = jnp.dot(piece, factor, preferred_element_type=jnp.float32)
        total = part if total is None else total + part
    return total


def per_device(density, density_mask, square_mask, result_mask, block_perm):
    groups = lax.axis_size("row")
    tile_blocks = density_mask.shape[0]
    width = density.shape[0] // tile_blocks
    half = width // lax.axis_size("layer")
    row_id = lax.axis_index("row")
    col_id = lax.axis_index("col")
    layer_id = lax.axis_index("layer")
    inverse = inverted(block_perm)

    masked = apply_pattern(density, density_mask)
    shaped = masked.reshape(tile_blocks, width, tile_blocks, width)
    shaped = jnp.take(shaped, group_order(block_perm, row_id, tile_blocks), axis=0)
    shaped = jnp.take(shaped, group_order(block_perm, col_id, tile_blocks), axis=2)
    pieces = shaped.transpose(0, 2, 1, 3).reshape(groups * groups, width, width)
    received = lax.all_to_all(pieces, ("row", "col"), split_axis=0, concat_axis=0, tiled=True)
    order = (source_groups(inverse, row_id, tile_blocks)[:, None] * groups
             + source_groups(inverse, col_id, tile_blocks)[None, :]).reshape(groups * groups)
    blocks = jnp.take(received, order, axis=0).reshape(groups, groups, width, width)
    grid_tile = blocks.transpose(0, 2, 1, 3).reshape(tile_blocks * width, tile_blocks * width)

    grid_half = lax.dynamic_index_in_dim(
        blocks.reshape(groups, groups, 2, half, width), layer_id, axis=2, keepdims=False
    ).transpose(0, 2, 1, 3).reshape(tile_blocks * half, tile_blocks * width)
    left = lax.all_gather(grid_half, "col", axis=0, tiled=False)
    right = gather_rows(grid_tile, row_id)
    right_stack = stack_pieces(right, groups)

    square_acc = jnp.einsum("gik,gkj->ij", left, right_stack, preferred_element_type=jnp.float32)
    square = apply_pattern(square_acc, square_mask).astype(jnp.bfloat16)

    cube = contract_left(gather_cols(square, col_id), right_stack)
    result = apply_pattern(3.0 * square.astype(jnp.float32) - 2.0 * cube, result_mask).astype(jnp.bfloat16)

    shaped = result.reshape(tile_blocks, half, tile_blocks, width)
    shaped = jnp.take(shaped, group_order(inverse, row_id, tile_blocks), axis=0)
    shaped = jnp.take(shaped, group_order(inverse, col_id, tile_blocks), axis=2)
    pieces = shaped.transpose(0, 2, 1, 3).reshape(groups * groups, half, width)
    pieces = jnp.concatenate([pieces, pieces], axis=0)
    returned = lax.all_to_all(pieces, ("layer", "row", "col"), split_axis=0, concat_axis=0, tiled=True)
    shaped = returned.reshape(2, groups, groups, half, width).transpose(1, 0, 3, 2, 4)
    shaped = shaped.reshape(groups, width, groups, width)
    shaped = jnp.take(shaped, source_groups(block_perm, row_id, tile_blocks), axis=0)
    shaped = jnp.take(shaped, source_groups(block_perm, col_id, tile_blocks), axis=2)
    return shaped.reshape(tile_blocks * width, tile_blocks * width)


def solution(mesh):
    in_specs = (P("row", "col"), P("row", "col"), P("row", "col"), P("row", "col"), P())
    out_specs = P("row", "col")
    return jax.shard_map(
        per_device, mesh=mesh, in_specs=in_specs, out_specs=out_specs, check_vma=False
    )
```

```python
import jax
import jax.numpy as jnp
from jax import lax
from jax.sharding import PartitionSpec as P


def apply_pattern(values, pattern):
    count = pattern.shape[0]
    rows = values.shape[0] // count
    cols = values.shape[1] // count
    shaped = values.reshape(count, rows, count, cols)
    shaped = shaped * pattern[:, None, :, None].astype(values.dtype)
    return shaped.reshape(count * rows, count * cols)


def inverted(mapping):
    positions = jnp.arange(mapping.shape[0], dtype=mapping.dtype)
    hits = mapping[None, :] == positions[:, None]
    return jnp.sum(jnp.where(hits, positions[None, :], 0), axis=1).astype(mapping.dtype)


def group_order(mapping, group, tile_blocks):
    return inverted(lax.dynamic_slice_in_dim(mapping, group * tile_blocks, tile_blocks) // tile_blocks)


def source_groups(mapping, group, tile_blocks):
    return lax.dynamic_slice_in_dim(mapping, group * tile_blocks, tile_blocks) // tile_blocks


def passed_along(array, axis, by):
    count = lax.axis_size(axis)
    return lax.ppermute(array, axis, [(i, (i + by) % count) for i in range(count)])


def partner_of(array, axis):
    count = lax.axis_size(axis)
    return lax.ppermute(array, axis, [(i, i ^ 1) for i in range(count)])


def gather_rows(tile, row_id):
    groups = lax.axis_size("row")
    size = tile.shape[0]
    below = passed_along(tile, "row", 2)
    above = passed_along(tile, "row", -2)
    far_top = passed_along(below[: size // 2], "row", 2)
    far_bottom = passed_along(above[size // 2 :], "row", -2)
    own = [(row_id, tile, 0), ((row_id - 2) % groups, below, 0), ((row_id + 2) % groups, above, 0),
           ((row_id + 4) % groups, far_top, 0), ((row_id + 4) % groups, far_bottom, size // 2)]
    shared = [((src ^ 1), partner_of(piece, "row"), first) for src, piece, first in own]
    return own + shared


def plane_move(array, by_x, swap_z):
    count = lax.axis_size("col")
    ring = count // 2
    pairs = []
    for i in range(count):
        z, x = divmod(i, ring)
        pairs.append((i, ((1 - z) if swap_z else z) * ring + (x + by_x) % ring))
    return lax.ppermute(array, "col", pairs)


def gather_cols(piece, col_id):
    count = lax.axis_size("col")
    ring = count // 2
    width = piece.shape[1]
    z, x = col_id // ring, col_id % ring

    def col(dz, dx):
        return ((z + dz) % 2) * ring + (x + dx) % ring

    across = plane_move(piece, 0, True)
    pieces = [(col(0, 0), piece, 0), (col(1, 0), across, 0)]
    for dz, start in ((0, piece), (1, across)):
        after = plane_move(start, 1, False)
        before = plane_move(start, -1, False)
        far_left = plane_move(after[:, : width // 2], 1, False)
        far_right = plane_move(before[:, width // 2 :], -1, False)
        pieces += [(col(dz, -1), after, 0), (col(dz, 1), before, 0),
                   (col(dz, 2), far_left, 0), (col(dz, 2), far_right, width // 2)]
    return pieces


def stack_pieces(pieces, groups):
    size = max(piece.shape[0] for _, piece, _ in pieces)
    stack = jnp.zeros((groups, size, pieces[0][1].shape[1]), pieces[0][1].dtype)
    for src, piece, first in pieces:
        stack = lax.dynamic_update_slice(stack, piece[None], (src, first, 0))
    return stack


def contract_left(pieces, stack):
    total = None
    for src, piece, first in pieces:
        factor = lax.dynamic_index_in_dim(stack, src, axis=0, keepdims=False)
        factor = factor[first : first + piece.shape[1]]
        part = jnp.dot(piece, factor, preferred_element_type=jnp.float32)
        total = part if total is None else total + part
    return total


def block_index(rows, cols, groups):
    return (rows[:, None] * groups + cols[None, :]).reshape(groups * groups)


def per_device(density, density_mask, square_mask, result_mask, block_perm):
    groups = lax.axis_size("row")
    tile_blocks = density_mask.shape[0]
    width = density.shape[0] // tile_blocks
    half = width // lax.axis_size("layer")
    row_id = lax.axis_index("row")
    col_id = lax.axis_index("col")
    layer_id = lax.axis_index("layer")
    inverse = inverted(block_perm)

    masked = apply_pattern(density, density_mask)
    blocks = masked.reshape(tile_blocks, width, tile_blocks, width).transpose(0, 2, 1, 3)
    blocks = blocks.reshape(tile_blocks * tile_blocks, width, width)
    pieces = jnp.take(blocks, block_index(group_order(block_perm, row_id, tile_blocks),
                                          group_order(block_perm, col_id, tile_blocks), groups), axis=0)
    received = lax.all_to_all(pieces, ("row", "col"), split_axis=0, concat_axis=0, tiled=True)
    order = block_index(source_groups(inverse, row_id, tile_blocks), source_groups(inverse, col_id, tile_blocks), groups)
    blocks = jnp.take(received, order, axis=0).reshape(groups, groups, width, width)
    grid_tile = blocks.transpose(0, 2, 1, 3).reshape(tile_blocks * width, tile_blocks * width)

    grid_half = lax.dynamic_index_in_dim(
        blocks.reshape(groups, groups, 2, half, width), layer_id, axis=2, keepdims=False
    ).transpose(0, 2, 1, 3).reshape(tile_blocks * half, tile_blocks * width)
    left = lax.all_gather(grid_half, "col", axis=0, tiled=False)
    right = gather_rows(grid_tile, row_id)
    right_stack = stack_pieces(right, groups)

    square_acc = jnp.einsum("gik,gkj->ij", left, right_stack, preferred_element_type=jnp.float32)
    square = apply_pattern(square_acc, square_mask).astype(jnp.bfloat16)

    cube = contract_left(gather_cols(square, col_id), right_stack)
    result = apply_pattern(3.0 * square.astype(jnp.float32) - 2.0 * cube, result_mask).astype(jnp.bfloat16)

    blocks = result.reshape(tile_blocks, half, tile_blocks, width).transpose(0, 2, 1, 3)
    blocks = blocks.reshape(tile_blocks * tile_blocks, half, width)
    pieces = jnp.take(blocks, block_index(group_order(inverse, row_id, tile_blocks),
                                          group_order(inverse, col_id, tile_blocks), groups), axis=0)
    pieces = jnp.concatenate([pieces, pieces], axis=0)
    returned = lax.all_to_all(pieces, ("layer", "row", "col"), split_axis=0, concat_axis=0, tiled=True)
    returned = jnp.take(returned.reshape(2, groups * groups, half, width),
                        block_index(source_groups(block_perm, row_id, tile_blocks),
                                    source_groups(block_perm, col_id, tile_blocks), groups), axis=1)
    shaped = returned.reshape(2, tile_blocks, tile_blocks, half, width).transpose(1, 0, 3, 2, 4)
    return shaped.reshape(tile_blocks * width, tile_blocks * width)


def solution(mesh):
    in_specs = (P("row", "col"), P("row", "col"), P("row", "col"), P("row", "col"), P())
    out_specs = P("row", "col")
    return jax.shard_map(
        per_device, mesh=mesh, in_specs=in_specs, out_specs=out_specs, check_vma=False
    )
```

```python
import jax
import jax.numpy as jnp
from jax import lax
from jax.sharding import PartitionSpec as P


def apply_pattern(values, pattern):
    count = pattern.shape[0]
    rows = values.shape[0] // count
    cols = values.shape[1] // count
    shaped = values.reshape(count, rows, count, cols)
    shaped = shaped * pattern[:, None, :, None].astype(values.dtype)
    return shaped.reshape(count * rows, count * cols)


def inverted(mapping):
    positions = jnp.arange(mapping.shape[0], dtype=mapping.dtype)
    hits = mapping[None, :] == positions[:, None]
    return jnp.sum(jnp.where(hits, positions[None, :], 0), axis=1).astype(mapping.dtype)


def group_order(mapping, group, tile_blocks):
    return inverted(lax.dynamic_slice_in_dim(mapping, group * tile_blocks, tile_blocks) // tile_blocks)


def source_groups(mapping, group, tile_blocks):
    return lax.dynamic_slice_in_dim(mapping, group * tile_blocks, tile_blocks) // tile_blocks


def passed_along(array, axis, by):
    count = lax.axis_size(axis)
    return lax.ppermute(array, axis, [(i, (i + by) % count) for i in range(count)])


def partner_of(array, axis):
    count = lax.axis_size(axis)
    return lax.ppermute(array, axis, [(i, i ^ 1) for i in range(count)])


def gather_rows(tile, row_id):
    groups = lax.axis_size("row")
    size = tile.shape[0]
    below = passed_along(tile, "row", 2)
    above = passed_along(tile, "row", -2)
    far_top = passed_along(below[: size // 2], "row", 2)
    far_bottom = passed_along(above[size // 2 :], "row", -2)
    own = [(row_id, tile, 0), ((row_id - 2) % groups, below, 0), ((row_id + 2) % groups, above, 0),
           ((row_id + 4) % groups, far_top, 0), ((row_id + 4) % groups, far_bottom, size // 2)]
    shared = [((src ^ 1), partner_of(piece, "row"), first) for src, piece, first in own]
    return own + shared


def plane_move(array, by_x, swap_z):
    count = lax.axis_size("col")
    ring = count // 2
    pairs = []
    for i in range(count):
        z, x = divmod(i, ring)
        pairs.append((i, ((1 - z) if swap_z else z) * ring + (x + by_x) % ring))
    return lax.ppermute(array, "col", pairs)


def gather_cols(piece, col_id):
    count = lax.axis_size("col")
    ring = count // 2
    width = piece.shape[1]
    z, x = col_id // ring, col_id % ring

    def col(dz, dx):
        return ((z + dz) % 2) * ring + (x + dx) % ring

    across = plane_move(piece, 0, True)
    pieces = [(col(0, 0), piece, 0), (col(1, 0), across, 0)]
    for dz, start in ((0, piece), (1, across)):
        after = plane_move(start, 1, False)
        before = plane_move(start, -1, False)
        far_left = plane_move(after[:, : width // 2], 1, False)
        far_right = plane_move(before[:, width // 2 :], -1, False)
        pieces += [(col(dz, -1), after, 0), (col(dz, 1), before, 0),
                   (col(dz, 2), far_left, 0), (col(dz, 2), far_right, width // 2)]
    return pieces


def stack_pieces(pieces, groups):
    size = max(piece.shape[0] for _, piece, _ in pieces)
    stack = jnp.zeros((groups, size, pieces[0][1].shape[1]), pieces[0][1].dtype)
    for src, piece, first in pieces:
        stack = lax.dynamic_update_slice(stack, piece[None], (src, first, 0))
    return stack


def contract_left(pieces, stack):
    total = None
    for src, piece, first in pieces:
        factor = lax.dynamic_index_in_dim(stack, src, axis=0, keepdims=False)
        factor = factor[first : first + piece.shape[1]]
        part = jnp.dot(piece, factor, preferred_element_type=jnp.float32)
        total = part if total is None else total + part
    return total


def block_index(rows, cols, groups):
    return (rows[:, None] * groups + cols[None, :]).reshape(groups * groups)


def per_device(density, density_mask, square_mask, result_mask, block_perm):
    groups = lax.axis_size("row")
    tile_blocks = density_mask.shape[0]
    width = density.shape[0] // tile_blocks
    half = width // lax.axis_size("layer")
    row_id = lax.axis_index("row")
    col_id = lax.axis_index("col")
    layer_id = lax.axis_index("layer")
    inverse = inverted(block_perm)

    masked = apply_pattern(density, density_mask)
    blocks = masked.reshape(tile_blocks, width, tile_blocks, width).transpose(0, 2, 1, 3)
    blocks = blocks.reshape(tile_blocks * tile_blocks, width, width)
    pieces = jnp.take(blocks, block_index(group_order(block_perm, row_id, tile_blocks),
                                          group_order(block_perm, col_id, tile_blocks), groups), axis=0)
    received = lax.all_to_all(pieces, ("row", "col"), split_axis=0, concat_axis=0, tiled=True)
    order = block_index(source_groups(inverse, row_id, tile_blocks), source_groups(inverse, col_id, tile_blocks), groups)
    blocks = jnp.take(received, order, axis=0).reshape(groups, groups, width, width)
    grid_tile = blocks.transpose(0, 2, 1, 3).reshape(tile_blocks * width, tile_blocks * width)

    grid_half = lax.dynamic_index_in_dim(
        blocks.reshape(groups, groups, 2, half, width), layer_id, axis=2, keepdims=False
    ).transpose(0, 2, 1, 3).reshape(tile_blocks * half, tile_blocks * width)
    left = lax.all_gather(grid_half, "col", axis=0, tiled=False)
    right = gather_rows(grid_tile, row_id)
    right_stack = stack_pieces(right, groups)

    square_acc = jnp.einsum("gik,gkj->ij", left, right_stack, preferred_element_type=jnp.float32)
    square = apply_pattern(square_acc, square_mask).astype(jnp.bfloat16)

    cube = contract_left(gather_cols(square, col_id), right_stack)
    result = apply_pattern(3.0 * square.astype(jnp.float32) - 2.0 * cube, result_mask).astype(jnp.bfloat16)

    blocks = result.reshape(tile_blocks, half, tile_blocks, width).transpose(0, 2, 1, 3)
    blocks = blocks.reshape(tile_blocks * tile_blocks, half, width)
    outgoing = block_index(group_order(inverse, row_id, tile_blocks), group_order(inverse, col_id, tile_blocks), groups)
    pieces = jnp.take(blocks, jnp.concatenate([outgoing, outgoing]), axis=0)
    returned = lax.all_to_all(pieces, ("layer", "row", "col"), split_axis=0, concat_axis=0, tiled=True)
    returned = jnp.take(returned.reshape(2, groups * groups, half, width),
                        block_index(source_groups(block_perm, row_id, tile_blocks),
                                    source_groups(block_perm, col_id, tile_blocks), groups), axis=1)
    shaped = returned.reshape(2, tile_blocks, tile_blocks, half, width).transpose(1, 0, 3, 2, 4)
    return shaped.reshape(tile_blocks * width, tile_blocks * width)


def solution(mesh):
    in_specs = (P("row", "col"), P("row", "col"), P("row", "col"), P("row", "col"), P())
    out_specs = P("row", "col")
    return jax.shard_map(
        per_device, mesh=mesh, in_specs=in_specs, out_specs=out_specs, check_vma=False
    )
```

```python
import jax
import jax.numpy as jnp
from jax import lax
from jax.sharding import PartitionSpec as P


def apply_pattern(values, pattern):
    count = pattern.shape[0]
    rows = values.shape[0] // count
    cols = values.shape[1] // count
    shaped = values.reshape(count, rows, count, cols)
    shaped = shaped * pattern[:, None, :, None].astype(values.dtype)
    return shaped.reshape(count * rows, count * cols)


def inverted(mapping):
    positions = jnp.arange(mapping.shape[0], dtype=mapping.dtype)
    hits = mapping[None, :] == positions[:, None]
    return jnp.sum(jnp.where(hits, positions[None, :], 0), axis=1).astype(mapping.dtype)


def group_order(mapping, group, tile_blocks):
    return inverted(lax.dynamic_slice_in_dim(mapping, group * tile_blocks, tile_blocks) // tile_blocks)


def source_groups(mapping, group, tile_blocks):
    return lax.dynamic_slice_in_dim(mapping, group * tile_blocks, tile_blocks) // tile_blocks


def passed_along(array, axis, by):
    count = lax.axis_size(axis)
    return lax.ppermute(array, axis, [(i, (i + by) % count) for i in range(count)])


def partner_of(array, axis):
    count = lax.axis_size(axis)
    return lax.ppermute(array, axis, [(i, i ^ 1) for i in range(count)])


def gather_rows(tile, row_id):
    groups = lax.axis_size("row")
    size = tile.shape[0]
    below = passed_along(tile, "row", 2)
    above = passed_along(tile, "row", -2)
    far_top = passed_along(below[: size // 2], "row", 2)
    far_bottom = passed_along(above[size // 2 :], "row", -2)
    own = [(row_id, tile, 0), ((row_id - 2) % groups, below, 0), ((row_id + 2) % groups, above, 0),
           ((row_id + 4) % groups, far_top, 0), ((row_id + 4) % groups, far_bottom, size // 2)]
    shared = [((src ^ 1), partner_of(piece, "row"), first) for src, piece, first in own]
    return own + shared


def plane_move(array, by_x, swap_z):
    count = lax.axis_size("col")
    ring = count // 2
    pairs = []
    for i in range(count):
        z, x = divmod(i, ring)
        pairs.append((i, ((1 - z) if swap_z else z) * ring + (x + by_x) % ring))
    return lax.ppermute(array, "col", pairs)


def gather_cols(piece, col_id):
    count = lax.axis_size("col")
    ring = count // 2
    width = piece.shape[1]
    z, x = col_id // ring, col_id % ring

    def col(dz, dx):
        return ((z + dz) % 2) * ring + (x + dx) % ring

    half = width // 2
    across = plane_move(piece, 0, True)
    after = plane_move(piece, 1, False)
    before = plane_move(piece, -1, False)
    far_left = plane_move(after[:, :half], 1, False)
    far_right = plane_move(before[:, half:], -1, False)
    across_after = plane_move(across[:, :half], 1, False)
    across_before = plane_move(across[:, half:], -1, False)
    partner_after = plane_move(after[:, half:], 0, True)
    partner_before = plane_move(before[:, :half], 0, True)
    across_far_left = plane_move(across_after, 1, False)
    across_far_right = plane_move(across_before, -1, False)
    return [(col(0, 0), piece, 0), (col(1, 0), across, 0), (col(0, -1), after, 0), (col(0, 1), before, 0),
            (col(0, 2), far_left, 0), (col(0, 2), far_right, half),
            (col(1, -1), across_after, 0), (col(1, -1), partner_after, half),
            (col(1, 1), across_before, half), (col(1, 1), partner_before, 0),
            (col(1, 2), across_far_left, 0), (col(1, 2), across_far_right, half)]


def stack_pieces(pieces, groups):
    size = max(piece.shape[0] for _, piece, _ in pieces)
    stack = jnp.zeros((groups, size, pieces[0][1].shape[1]), pieces[0][1].dtype)
    for src, piece, first in pieces:
        stack = lax.dynamic_update_slice(stack, piece[None], (src, first, 0))
    return stack


def contract_left(pieces, stack):
    total = None
    for src, piece, first in pieces:
        factor = lax.dynamic_index_in_dim(stack, src, axis=0, keepdims=False)
        factor = factor[first : first + piece.shape[1]]
        part = jnp.dot(piece, factor, preferred_element_type=jnp.float32)
        total = part if total is None else total + part
    return total


def block_index(rows, cols, groups):
    return (rows[:, None] * groups + cols[None, :]).reshape(groups * groups)


def per_device(density, density_mask, square_mask, result_mask, block_perm):
    groups = lax.axis_size("row")
    tile_blocks = density_mask.shape[0]
    width = density.shape[0] // tile_blocks
    half = width // lax.axis_size("layer")
    row_id = lax.axis_index("row")
    col_id = lax.axis_index("col")
    layer_id = lax.axis_index("layer")
    inverse = inverted(block_perm)

    masked = apply_pattern(density, density_mask)
    blocks = masked.reshape(tile_blocks, width, tile_blocks, width).transpose(0, 2, 1, 3)
    blocks = blocks.reshape(tile_blocks * tile_blocks, width, width)
    pieces = jnp.take(blocks, block_index(group_order(block_perm, row_id, tile_blocks),
                                          group_order(block_perm, col_id, tile_blocks), groups), axis=0)
    received = lax.all_to_all(pieces, ("row", "col"), split_axis=0, concat_axis=0, tiled=True)
    order = block_index(source_groups(inverse, row_id, tile_blocks), source_groups(inverse, col_id, tile_blocks), groups)
    blocks = jnp.take(received, order, axis=0).reshape(groups, groups, width, width)
    grid_tile = blocks.transpose(0, 2, 1, 3).reshape(tile_blocks * width, tile_blocks * width)

    grid_half = lax.dynamic_index_in_dim(
        blocks.reshape(groups, groups, 2, half, width), layer_id, axis=2, keepdims=False
    ).transpose(0, 2, 1, 3).reshape(tile_blocks * half, tile_blocks * width)
    left = lax.all_gather(grid_half, "col", axis=0, tiled=False)
    right = gather_rows(grid_tile, row_id)
    right_stack = stack_pieces(right, groups)

    square_acc = jnp.einsum("gik,gkj->ij", left, right_stack, preferred_element_type=jnp.float32)
    square = apply_pattern(square_acc, square_mask).astype(jnp.bfloat16)

    cube = contract_left(gather_cols(square, col_id), right_stack)
    result = apply_pattern(3.0 * square.astype(jnp.float32) - 2.0 * cube, result_mask).astype(jnp.bfloat16)

    blocks = result.reshape(tile_blocks, half, tile_blocks, width).transpose(0, 2, 1, 3)
    blocks = blocks.reshape(tile_blocks * tile_blocks, half, width)
    outgoing = block_index(group_order(inverse, row_id, tile_blocks), group_order(inverse, col_id, tile_blocks), groups)
    pieces = jnp.take(blocks, jnp.concatenate([outgoing, outgoing]), axis=0)
    returned = lax.all_to_all(pieces, ("layer", "row", "col"), split_axis=0, concat_axis=0, tiled=True)
    returned = jnp.take(returned.reshape(2, groups * groups, half, width),
                        block_index(source_groups(block_perm, row_id, tile_blocks),
                                    source_groups(block_perm, col_id, tile_blocks), groups), axis=1)
    shaped = returned.reshape(2, tile_blocks, tile_blocks, half, width).transpose(1, 0, 3, 2, 4)
    return shaped.reshape(tile_blocks * width, tile_blocks * width)


def solution(mesh):
    in_specs = (P("row", "col"), P("row", "col"), P("row", "col"), P("row", "col"), P())
    out_specs = P("row", "col")
    return jax.shard_map(
        per_device, mesh=mesh, in_specs=in_specs, out_specs=out_specs, check_vma=False
    )
```

```python
import jax
import jax.numpy as jnp
from jax import lax
from jax.sharding import PartitionSpec as P


def apply_pattern(values, pattern):
    count = pattern.shape[0]
    rows = values.shape[0] // count
    cols = values.shape[1] // count
    shaped = values.reshape(count, rows, count, cols)
    shaped = shaped * pattern[:, None, :, None].astype(values.dtype)
    return shaped.reshape(count * rows, count * cols)


def inverted(mapping):
    positions = jnp.arange(mapping.shape[0], dtype=mapping.dtype)
    hits = mapping[None, :] == positions[:, None]
    return jnp.sum(jnp.where(hits, positions[None, :], 0), axis=1).astype(mapping.dtype)


def group_order(mapping, group, tile_blocks):
    return inverted(lax.dynamic_slice_in_dim(mapping, group * tile_blocks, tile_blocks) // tile_blocks)


def source_groups(mapping, group, tile_blocks):
    return lax.dynamic_slice_in_dim(mapping, group * tile_blocks, tile_blocks) // tile_blocks


def passed_along(array, axis, by):
    count = lax.axis_size(axis)
    return lax.ppermute(array, axis, [(i, (i + by) % count) for i in range(count)])


def partner_of(array, axis):
    count = lax.axis_size(axis)
    return lax.ppermute(array, axis, [(i, i ^ 1) for i in range(count)])


def gather_rows(tile, row_id):
    groups = lax.axis_size("row")
    size = tile.shape[0]
    below = passed_along(tile, "row", 2)
    above = passed_along(tile, "row", -2)
    far_top = passed_along(below[: size // 2], "row", 2)
    far_bottom = passed_along(above[size // 2 :], "row", -2)
    own = [(row_id, tile, 0), ((row_id - 2) % groups, below, 0), ((row_id + 2) % groups, above, 0),
           ((row_id + 4) % groups, far_top, 0), ((row_id + 4) % groups, far_bottom, size // 2)]
    partner = row_id ^ 1
    near = partner_of(jnp.concatenate([below, above]), "row")
    far = partner_of(jnp.concatenate([far_top, far_bottom]), "row")
    shared = [(partner, partner_of(tile, "row"), 0),
              ((partner - 2) % groups, near[:size], 0), ((partner + 2) % groups, near[size:], 0),
              ((partner + 4) % groups, far, 0)]
    return own + shared


def plane_move(array, by_x, swap_z):
    count = lax.axis_size("col")
    ring = count // 2
    pairs = []
    for i in range(count):
        z, x = divmod(i, ring)
        pairs.append((i, ((1 - z) if swap_z else z) * ring + (x + by_x) % ring))
    return lax.ppermute(array, "col", pairs)


def gather_cols(piece, col_id):
    count = lax.axis_size("col")
    ring = count // 2
    width = piece.shape[1]
    z, x = col_id // ring, col_id % ring

    def col(dz, dx):
        return ((z + dz) % 2) * ring + (x + dx) % ring

    half = width // 2
    across = plane_move(piece, 0, True)
    after = plane_move(piece, 1, False)
    before = plane_move(piece, -1, False)
    far_left = plane_move(after[:, :half], 1, False)
    far_right = plane_move(before[:, half:], -1, False)
    across_after = plane_move(across[:, :half], 1, False)
    across_before = plane_move(across[:, half:], -1, False)
    partner_after = plane_move(after[:, half:], 0, True)
    partner_before = plane_move(before[:, :half], 0, True)
    across_far_left = plane_move(across_after, 1, False)
    across_far_right = plane_move(across_before, -1, False)
    return [(col(0, 0), piece, 0), (col(1, 0), across, 0), (col(0, -1), after, 0), (col(0, 1), before, 0),
            (col(0, 2), far_left, 0), (col(0, 2), far_right, half),
            (col(1, -1), across_after, 0), (col(1, -1), partner_after, half),
            (col(1, 1), across_before, half), (col(1, 1), partner_before, 0),
            (col(1, 2), across_far_left, 0), (col(1, 2), across_far_right, half)]


def stack_pieces(pieces, groups):
    size = max(piece.shape[0] for _, piece, _ in pieces)
    stack = jnp.zeros((groups, size, pieces[0][1].shape[1]), pieces[0][1].dtype)
    for src, piece, first in pieces:
        stack = lax.dynamic_update_slice(stack, piece[None], (src, first, 0))
    return stack


def contract_left(pieces, stack):
    total = None
    for src, piece, first in pieces:
        factor = lax.dynamic_index_in_dim(stack, src, axis=0, keepdims=False)
        factor = factor[first : first + piece.shape[1]]
        part = jnp.dot(piece, factor, preferred_element_type=jnp.float32)
        total = part if total is None else total + part
    return total


def block_index(rows, cols, groups):
    return (rows[:, None] * groups + cols[None, :]).reshape(groups * groups)


def per_device(density, density_mask, square_mask, result_mask, block_perm):
    groups = lax.axis_size("row")
    tile_blocks = density_mask.shape[0]
    width = density.shape[0] // tile_blocks
    half = width // lax.axis_size("layer")
    row_id = lax.axis_index("row")
    col_id = lax.axis_index("col")
    layer_id = lax.axis_index("layer")
    inverse = inverted(block_perm)

    masked = apply_pattern(density, density_mask)
    blocks = masked.reshape(tile_blocks, width, tile_blocks, width).transpose(0, 2, 1, 3)
    blocks = blocks.reshape(tile_blocks * tile_blocks, width, width)
    pieces = jnp.take(blocks, block_index(group_order(block_perm, row_id, tile_blocks),
                                          group_order(block_perm, col_id, tile_blocks), groups), axis=0)
    received = lax.all_to_all(pieces, ("row", "col"), split_axis=0, concat_axis=0, tiled=True)
    order = block_index(source_groups(inverse, row_id, tile_blocks), source_groups(inverse, col_id, tile_blocks), groups)
    blocks = jnp.take(received, order, axis=0).reshape(groups, groups, width, width)
    grid_tile = blocks.transpose(0, 2, 1, 3).reshape(tile_blocks * width, tile_blocks * width)

    grid_half = lax.dynamic_index_in_dim(
        blocks.reshape(groups, groups, 2, half, width), layer_id, axis=2, keepdims=False
    ).transpose(0, 2, 1, 3).reshape(tile_blocks * half, tile_blocks * width)
    left = lax.all_gather(grid_half, "col", axis=0, tiled=False)
    right = gather_rows(grid_tile, row_id)
    right_stack = stack_pieces(right, groups)

    square_acc = jnp.einsum("gik,gkj->ij", left, right_stack, preferred_element_type=jnp.float32)
    square = apply_pattern(square_acc, square_mask).astype(jnp.bfloat16)

    cube = contract_left(gather_cols(square, col_id), right_stack)
    result = apply_pattern(3.0 * square.astype(jnp.float32) - 2.0 * cube, result_mask).astype(jnp.bfloat16)

    blocks = result.reshape(tile_blocks, half, tile_blocks, width).transpose(0, 2, 1, 3)
    blocks = blocks.reshape(tile_blocks * tile_blocks, half, width)
    outgoing = block_index(group_order(inverse, row_id, tile_blocks), group_order(inverse, col_id, tile_blocks), groups)
    pieces = jnp.take(blocks, jnp.concatenate([outgoing, outgoing]), axis=0)
    returned = lax.all_to_all(pieces, ("layer", "row", "col"), split_axis=0, concat_axis=0, tiled=True)
    returned = jnp.take(returned.reshape(2, groups * groups, half, width),
                        block_index(source_groups(block_perm, row_id, tile_blocks),
                                    source_groups(block_perm, col_id, tile_blocks), groups), axis=1)
    shaped = returned.reshape(2, tile_blocks, tile_blocks, half, width).transpose(1, 0, 3, 2, 4)
    return shaped.reshape(tile_blocks * width, tile_blocks * width)


def solution(mesh):
    in_specs = (P("row", "col"), P("row", "col"), P("row", "col"), P("row", "col"), P())
    out_specs = P("row", "col")
    return jax.shard_map(
        per_device, mesh=mesh, in_specs=in_specs, out_specs=out_specs, check_vma=False
    )
```
